32 devices in a mesh: groups: 2 (over x), ctx: 16 (over z, y, core).
Axes of the slice: x: 2, y: 2, z: 4, core: 2. Of those that a mesh axis runs over, the one named last changes fastest.
Arguments:
- sem_queries: bfloat16 [8192, 1024], P(('groups', 'ctx')), parts along dimension 0, may hold values from -170 to 170
- sem_keys: bfloat16 [8192, 1024], P(('groups', 'ctx')), parts along dimension 0, may hold values from -7 to 7
- sem_values: bfloat16 [8192, 1024], P(('groups', 'ctx')), parts along dimension 0, may hold values from -6 to 6
- sem_inputs: bfloat16 [8192, 2048], P(('groups', 'ctx')), parts along dimension 0, may hold values from -80 to 80
- out_proj: bfloat16 [1024, 2048], P('ctx'), may hold values from -0.5 to 0.5
- norm_gain: float32 [2048], replicated, may hold values from 0.1 to 1.9
- key_proj: bfloat16 [2048, 1024], P('ctx'), may hold values from -0.125 to 0.125
- value_proj: bfloat16 [2048, 1024], P('ctx'), may hold values from -0.125 to 0.125
- slopes: float32 [8], replicated, may hold values from 1 to 16
- coarse_queries: bfloat16 [32768, 1024], P(('groups', 'ctx')), parts along dimension 0, may hold values from -400 to 400
- counts: int32 [32], P(('groups', 'ctx')), parts along dimension 0, may hold values from 512 to 1024, as said below
- band_bounds: int32 [128, 2], P(('groups', 'ctx')), parts along dimension 0, may hold values from 0 to 4096, as said below
Outputs:
- coarse_context: bfloat16 [32768, 1024], P(('groups', 'ctx')), parts along dimension 0
The draws below stay inside these ranges and needn't reach their ends.
There are 2 independent parts, one for each index of `groups`. The reference program is written for one: setup_inputs(seed, part) draws one part's arguments, and reference() takes and returns one part's arrays. A program takes and returns all parts, laid end to end along the dimension named above; an argument that names none is the same for every part. Nothing has to cross between parts.
Inputs may be any that keep to these rules, and one draw needn't show every extreme that they name: `counts`: live coarse tokens of a ctx index fill its first slots; at least half of 1024; some index is full. `band_bounds`: a band of block n, held by ctx index c = n // 4, covers 512 // 2 to 512 rows and lies within the semantic rows of indices c - 1, c and c + 1; block 0 covers exactly 512.
All inputs are finite; a program needn't handle non-finite values.
Results may differ from the reference program's by a relative error of at most 0.0091.
Values may be sent and summed in bfloat16 or wider, within the bound.
No kernel may reach another device: no remote copies, remote signals or barrier semaphores. Data moves between devices by JAX's collectives and lax.ppermute only.
A program may use at most 128 MiB of HBM per device.

```python
import math
import jax
import jax.numpy as jnp
from jax import lax

D = 2048
HEADS = 8
HEAD_DIM = 128
S_DEV = 256
W = 512
BAND = 512
CB = 256
HD = 1024
S_TOTAL = 4096
C_DEV = 1024
NB = 4
C_TOTAL = 16384


def paired_keys(key):
    key_base = jax.random.truncated_normal(jax.random.fold_in(key, 11), -6.0, 6.0, (S_TOTAL, HD), jnp.float32)
    query_base = jax.random.truncated_normal(jax.random.fold_in(key, 12), -6.0, 6.0, (S_TOTAL, HD), jnp.float32)
    return (query_base, key_base)


def draw_sem_queries(key, part):
    return paired_keys(key)[0].astype(jnp.bfloat16)


def draw_sem_keys(key, part):
    return paired_keys(key)[1].astype(jnp.bfloat16)


def draw_sem_inputs(key, part):
    base = jax.random.truncated_normal(jax.random.fold_in(key, 21), -4.0, 4.0, (S_TOTAL, D), jnp.float32)
    row_scale = jnp.exp(jax.random.uniform(jax.random.fold_in(key, 22), (S_TOTAL, 1), jnp.float32, -1.2, 1.1))
    column_scale = jnp.exp(jax.random.uniform(jax.random.fold_in(key, 23), (1, D), jnp.float32, -1.2, 1.1))
    return (base * row_scale * column_scale).astype(jnp.bfloat16)


def draw_coarse_queries(key, part):
    base = jax.random.truncated_normal(jax.random.fold_in(key, 41), -6.0, 6.0, (C_TOTAL, HD), jnp.float32)
    return base.astype(jnp.bfloat16)


def coarse_layout(key):
    device_total = S_TOTAL // S_DEV
    counts = jax.random.randint(jax.random.fold_in(key, 31), (device_total,), C_DEV // 2, C_DEV + 1)
    full_device = jax.random.randint(jax.random.fold_in(key, 32), (), 0, device_total)
    devices = jnp.arange(device_total)
    counts = jnp.where(devices == full_device, C_DEV, counts).astype(jnp.int32)
    starts = (jnp.cumsum(counts) - counts).astype(jnp.int32)
    blocks = jnp.arange(device_total * NB)
    owner_device = blocks // NB
    first_pos = starts[owner_device] + blocks % NB * CB
    center = (first_pos // 2 + CB // 4) * 2 // 3
    length = jax.random.randint(jax.random.fold_in(key, 33), (device_total * NB,), BAND // 2, BAND + 1)
    length = jnp.where(blocks == 0, BAND, length)
    jitter = jax.random.randint(jax.random.fold_in(key, 34), (device_total * NB,), -(BAND // 4), BAND // 4 + 1)
    lowest = jnp.maximum(owner_device - 1, 0) * S_DEV
    highest = jnp.minimum(owner_device + 2, device_total) * S_DEV
    band_low = jnp.clip(center - length // 2 + jitter, lowest, highest - length)
    return (counts, jnp.stack([band_low, band_low + length], axis=1).astype(jnp.int32))


def draw_counts(key, part):
    return coarse_layout(key)[0]


def draw_band_bounds(key, part):
    return coarse_layout(key)[1]


def shard_levels(key, dims, split, low, top_value):
    level, own = 1.0, jax.random.fold_in(key, 6)
    for position, shards_of in split:
        draws = jnp.exp(jax.random.uniform(jax.random.fold_in(own, position), (shards_of,), jnp.float32, low / len(split), top_value / len(split)))
        level = level * jnp.repeat(draws, dims[position] // shards_of).reshape([-1 if axis == position else 1 for axis in range(len(dims))])
    return level


def bell_draw(stream_key, dims, width, limit, cuts=(), kind=jnp.bfloat16):
    drawn = width * jax.random.normal(stream_key, dims, jnp.float32)
    if cuts:
        drawn = drawn * shard_levels(stream_key, dims, cuts, -0.22, 0.18)
    return jnp.clip(drawn, -limit, limit).astype(kind)


def setup_inputs(seed: int = 0, part: int = 0) -> dict:
    seeds = jax.random.split(jax.random.key(seed), 13)
    part_keys = jax.random.split(jax.random.fold_in(seeds[12], part), 13)
    sem_queries = draw_sem_queries(jax.random.fold_in(jax.random.fold_in(seeds[12], part), 71), part)
    sem_keys = draw_sem_keys(jax.random.fold_in(jax.random.fold_in(seeds[12], part), 71), part)
    sem_values = bell_draw(part_keys[2], (S_TOTAL, HD), 1.0, 6.0, ((0, 16),))
    sem_inputs = draw_sem_inputs(jax.random.fold_in(jax.random.fold_in(seeds[12], part), 71), part)
    out_proj = bell_draw(seeds[4], (HD, D), HEAD_DIM ** -0.5, 0.5, ((0, 16),))
    norm_gain = jnp.clip(1.0 + 0.18 * jax.random.normal(seeds[5], (D,), jnp.float32), 0.1, 1.9)
    key_proj = bell_draw(seeds[6], (D, HD), D ** -0.5, 0.125, ((0, 16),))
    value_proj = bell_draw(seeds[7], (D, HD), D ** -0.5, 0.125, ((0, 16),))
    slopes = jnp.clip(jnp.exp(jax.random.uniform(seeds[8], (HEADS,), jnp.float32, math.log(1.0), math.log(16.0))), 1.0, 16.0)
    coarse_queries = draw_coarse_queries(jax.random.fold_in(jax.random.fold_in(seeds[12], part), 71), part)
    counts = draw_counts(jax.random.fold_in(jax.random.fold_in(seeds[12], part), 71), part)
    band_bounds = draw_band_bounds(jax.random.fold_in(jax.random.fold_in(seeds[12], part), 71), part)
    return dict(sem_queries=sem_queries, sem_keys=sem_keys, sem_values=sem_values, sem_inputs=sem_inputs, out_proj=out_proj, norm_gain=norm_gain, key_proj=key_proj, value_proj=value_proj, slopes=slopes, coarse_queries=coarse_queries, counts=counts, band_bounds=band_bounds)


NEG_FILL = -1e+30

def head_split(matrix):
    return matrix.reshape(matrix.shape[0], HEADS, HEAD_DIM)

def attend(queries, key_rows, value_rows, allowed, time_bias):
    scores = jnp.einsum('qhd,khd->hqk', head_split(queries).astype(jnp.float32), head_split(key_rows).astype(jnp.float32)) * HEAD_DIM ** (-0.5)
    scores = jnp.where(allowed[None], scores + time_bias, NEG_FILL)
    largest = lax.optimization_barrier(jnp.max(scores, axis=2, keepdims=True))
    exponent = jnp.exp(scores - largest)
    weights = (exponent / lax.optimization_barrier(jnp.sum(exponent, axis=2, keepdims=True))).astype(jnp.bfloat16)
    blended = jnp.einsum('hqk,khd->qhd', weights.astype(jnp.float32), head_split(value_rows).astype(jnp.float32))
    return blended.reshape(queries.shape[0], -1)

def normalize(sem_stream, norm_gain):
    scaled = sem_stream * lax.rsqrt(lax.optimization_barrier(jnp.mean(sem_stream * sem_stream, axis=1, keepdims=True)) + 1e-05)
    return (scaled * norm_gain[None, :]).astype(jnp.bfloat16)

def cross_attend(queries, key_rows, value_rows, key_global, band_low, band_high, positions, slopes, live_rows):
    timing = (positions // 2).astype(jnp.float32) * (2.0 / 3.0)
    distance = jnp.abs(timing[:, None] - key_global[None, :].astype(jnp.float32))
    time_bias = -slopes[:, None, None] * distance[None] / BAND
    inside = (key_global >= band_low) & (key_global < band_high)
    allowed = jnp.broadcast_to(inside[None, :], (queries.shape[0], key_global.shape[0]))
    blended = attend(queries, key_rows, value_rows, allowed, time_bias)
    return jnp.where(live_rows[:, None], blended, 0.0).astype(jnp.bfloat16)

def reference(sem_queries, sem_keys, sem_values, sem_inputs, out_proj, norm_gain, key_proj, value_proj, slopes, coarse_queries, counts, band_bounds):
    padded_keys = jnp.concatenate([jnp.zeros((W, HD), jnp.bfloat16), sem_keys], axis=0)
    padded_values = jnp.concatenate([jnp.zeros((W, HD), jnp.bfloat16), sem_values], axis=0)

    def sem_block(block_index):
        first_row = block_index * S_DEV
        queries = lax.dynamic_slice_in_dim(sem_queries, first_row, S_DEV, 0)
        key_rows = lax.dynamic_slice_in_dim(padded_keys, first_row, S_DEV + W, 0)
        value_rows = lax.dynamic_slice_in_dim(padded_values, first_row, S_DEV + W, 0)
        query_global = first_row + jnp.arange(S_DEV, dtype=jnp.int32)
        key_global = first_row - W + jnp.arange(S_DEV + W, dtype=jnp.int32)
        key_lag = query_global[:, None] - key_global[None, :]
        allowed = (key_lag >= 0) & (key_lag < W) & (key_global[None, :] >= 0)
        return attend(queries, key_rows, value_rows, allowed, 0.0).astype(jnp.bfloat16)
    sem_att = lax.map(sem_block, jnp.arange(S_TOTAL // S_DEV, dtype=jnp.int32)).reshape(S_TOTAL, HD)
    sem_stream = sem_inputs.astype(jnp.float32) + jnp.dot(sem_att, out_proj, preferred_element_type=jnp.float32)
    normed = normalize(sem_stream, norm_gain)
    cross_keys = jnp.dot(normed, key_proj, preferred_element_type=jnp.float32).astype(jnp.bfloat16)
    cross_values = jnp.dot(normed, value_proj, preferred_element_type=jnp.float32).astype(jnp.bfloat16)
    stream_starts = (jnp.cumsum(counts) - counts).astype(jnp.int32)

    def coarse_block(block_index):
        owner_device = block_index // NB
        row_local = block_index % NB * CB + jnp.arange(CB, dtype=jnp.int32)
        band_low = band_bounds[block_index, 0]
        band_high = band_bounds[block_index, 1]
        first_key = jnp.minimum(band_low, S_TOTAL - BAND).astype(jnp.int32)
        key_rows = lax.dynamic_slice_in_dim(cross_keys, first_key, BAND, 0)
        value_rows = lax.dynamic_slice_in_dim(cross_values, first_key, BAND, 0)
        key_global = first_key + jnp.arange(BAND, dtype=jnp.int32)
        queries = lax.dynamic_slice_in_dim(coarse_queries, (block_index * CB).astype(jnp.int32), CB, 0)
        positions = stream_starts[owner_device] + row_local
        return cross_attend(queries, key_rows, value_rows, key_global, band_low, band_high, positions, slopes, row_local < counts[owner_device])
    return lax.map(coarse_block, jnp.arange(C_TOTAL // CB, dtype=jnp.int32)).reshape(C_TOTAL, HD)
```

```python
import functools

import jax
import jax.numpy as jnp
from jax import lax
from jax.experimental import pallas as pl
from jax.experimental.pallas import tpu as pltpu
from jax.sharding import PartitionSpec as P

HEADS = 8
HEAD_DIM = 128
W = 512
BAND = 512
CB = 256


NEG_FILL = -1e30


def passed_along(array, axis, by):
    length = lax.axis_size(axis)
    pairs = [(i, i + by) for i in range(length) if 0 <= i + by < length]
    return lax.ppermute(array, axis, pairs)


def with_halo(array, sides, width):
    for axis, dim in sides:
        size, length = (lax.axis_size(axis), array.shape[dim])
        up = [(i, (i + 1) % size) for i in range(size - 1)]
        down = [(j, i) for i, j in up]
        last = lax.slice_in_dim(array, length - width, length, axis=dim)
        first = lax.slice_in_dim(array, 0, width, axis=dim)
        before = lax.ppermute(last, axis, up)
        after = lax.ppermute(first, axis, down)
        array = jnp.concatenate([before, array, after], axis=dim)
    return array


def head_split(matrix):
    return matrix.reshape(matrix.shape[0], HEADS, HEAD_DIM)


def attend(queries, key_rows, value_rows, allowed, time_bias):
    scores = jnp.einsum(
        "qhd,khd->hqk",
        head_split(queries),
        head_split(key_rows),
        preferred_element_type=jnp.float32,
    ) * HEAD_DIM ** (-0.5)
    scores = jnp.where(allowed[None], scores + time_bias, NEG_FILL)
    largest = jnp.max(scores, axis=2, keepdims=True)
    exponent = jnp.exp(scores - largest)
    weights = (exponent / jnp.sum(exponent, axis=2, keepdims=True)).astype(jnp.bfloat16)
    blended = jnp.einsum(
        "hqk,khd->qhd", weights, head_split(value_rows), preferred_element_type=jnp.float32
    )
    return blended.reshape(queries.shape[0], -1)


def normalize(sem_stream, norm_gain):
    scaled = sem_stream * lax.rsqrt(
        jnp.mean(sem_stream * sem_stream, axis=1, keepdims=True) + 1e-05
    )
    return (scaled * norm_gain[None, :]).astype(jnp.bfloat16)


def contract_rows(left_side, weight_piece):
    return jnp.dot(left_side, weight_piece, preferred_element_type=jnp.float32)


def coarse_kernel(prm, slopes_ref, q_ref, k_ref, v_ref, o_ref, *, blocks, near_rows):
    n = pl.program_id(0)
    band_low = prm[2 * n]
    band_high = prm[2 * n + 1]
    stream_start = prm[2 * blocks]
    live_count = prm[2 * blocks + 1]
    base_row = prm[2 * blocks + 2]
    rows = n * CB + lax.broadcasted_iota(jnp.int32, (CB, 1), 0)
    timing = ((stream_start + rows) // 2).astype(jnp.float32) * (2.0 / 3.0)
    key_global = base_row + lax.broadcasted_iota(jnp.int32, (1, near_rows), 1)
    inside = (key_global >= band_low) & (key_global < band_high)
    distance = jnp.abs(timing - key_global.astype(jnp.float32))
    live_rows = rows < live_count
    for h in range(HEADS):
        cols = slice(h * HEAD_DIM, (h + 1) * HEAD_DIM)
        scores = lax.dot_general(
            q_ref[:, cols], k_ref[:, cols], (((1,), (1,)), ((), ())),
            preferred_element_type=jnp.float32,
        ) * HEAD_DIM ** (-0.5)
        time_bias = distance * (-slopes_ref[h] / BAND)
        scores = jnp.where(inside, scores + time_bias, NEG_FILL)
        largest = jnp.max(scores, axis=1, keepdims=True)
        exponent = jnp.exp(scores - largest)
        total = jnp.sum(exponent, axis=1, keepdims=True)
        weights = (exponent * (1.0 / total)).astype(jnp.bfloat16)
        blended = jnp.dot(weights, v_ref[:, cols], preferred_element_type=jnp.float32)
        o_ref[:, cols] = jnp.where(live_rows, blended, 0.0).astype(jnp.bfloat16)


def coarse_attention(coarse_queries, near_pair, params, slopes):
    slots, width = coarse_queries.shape
    blocks = slots // CB
    near_rows = near_pair.shape[1]
    kernel = functools.partial(coarse_kernel, blocks=blocks, near_rows=near_rows)
    grid_spec = pltpu.PrefetchScalarGridSpec(
        num_scalar_prefetch=1,
        grid=(blocks,),
        in_specs=[
            pl.BlockSpec(memory_space=pltpu.SMEM),
            pl.BlockSpec((CB, width), lambda n, prm: (n, 0)),
            pl.BlockSpec((None, near_rows, width), lambda n, prm: (0, 0, 0)),
            pl.BlockSpec((None, near_rows, width), lambda n, prm: (1, 0, 0)),
        ],
        out_specs=pl.BlockSpec((CB, width), lambda n, prm: (n, 0)),
    )
    return pl.pallas_call(
        kernel,
        grid_spec=grid_spec,
        out_shape=jax.ShapeDtypeStruct((slots, width), jnp.bfloat16),
        compiler_params=pltpu.CompilerParams(dimension_semantics=("arbitrary",)),
    )(params, slopes, coarse_queries, near_pair, near_pair)


def on_device(
    sem_queries,
    sem_keys,
    sem_values,
    sem_inputs,
    out_proj,
    norm_gain,
    key_proj,
    value_proj,
    slopes,
    coarse_queries,
    counts,
    band_bounds,
):
    rows_here = sem_queries.shape[0]
    device_index = lax.axis_index("ctx")
    ctx_size = lax.axis_size("ctx")
    full_out_proj = lax.all_gather(out_proj, "ctx", axis=0, tiled=True)
    cross_rows, cross_cols = key_proj.shape
    stacked_proj = jnp.stack([key_proj, value_proj])
    gathered_proj = lax.all_gather(stacked_proj, "ctx", axis=1, tiled=True)
    own_pair = jnp.stack([sem_keys, sem_values])
    reach_shards = (W - 1 + rows_here - 1) // rows_here
    earlier = []
    for distance in range(1, reach_shards + 1):
        earlier.insert(0, passed_along(own_pair, "ctx", distance))
    window_pair = jnp.concatenate(earlier + [own_pair], axis=1)
    query_pos = jnp.arange(rows_here, dtype=jnp.int32)
    key_pos = jnp.arange(window_pair.shape[1], dtype=jnp.int32)
    key_lag = query_pos[:, None] + reach_shards * rows_here - key_pos[None, :]
    key_global = device_index * rows_here - reach_shards * rows_here + key_pos
    allowed = (key_lag >= 0) & (key_lag < W) & (key_global[None, :] >= 0)
    sem_att = attend(sem_queries, window_pair[0], window_pair[1], allowed, 0.0).astype(jnp.bfloat16)
    projected = contract_rows(sem_att, full_out_proj)
    sem_stream = sem_inputs.astype(jnp.float32) + projected
    normed = normalize(sem_stream, norm_gain)
    key_sum = contract_rows(normed, gathered_proj[0])
    value_sum = contract_rows(normed, gathered_proj[1])
    cross_keys = key_sum.astype(jnp.bfloat16)
    cross_values = value_sum.astype(jnp.bfloat16)
    every_count = lax.all_gather(counts, "ctx", axis=0, tiled=True)
    earlier_index = jnp.arange(ctx_size, dtype=jnp.int32) < device_index
    stream_start = jnp.sum(jnp.where(earlier_index, every_count, 0)).astype(jnp.int32)
    near_pair = with_halo(jnp.stack([cross_keys, cross_values]), (("ctx", 1),), rows_here)
    base_row = (device_index - 1) * rows_here
    params = jnp.concatenate(
        [band_bounds.reshape(-1).astype(jnp.int32),
         jnp.stack([stream_start, counts[0], base_row]).astype(jnp.int32)]
    )
    return coarse_attention(coarse_queries, near_pair, params, slopes)


def solution(mesh):
    return jax.shard_map(
        on_device,
        mesh=mesh,
        in_specs=(
            P(("groups", "ctx"), None),
            P(("groups", "ctx"), None),
            P(("groups", "ctx"), None),
            P(("groups", "ctx"), None),
            P("ctx", None),
            P(),
            P("ctx", None),
            P("ctx", None),
            P(),
            P(("groups", "ctx"), None),
            P(("groups", "ctx")),
            P(("groups", "ctx"), None),
        ),
        out_specs=P(("groups", "ctx"), None),
        check_vma=False,
    )
```

```python
import functools

import jax
import jax.numpy as jnp
from jax import lax
from jax.experimental import pallas as pl
from jax.experimental.pallas import tpu as pltpu
from jax.sharding import PartitionSpec as P

HEADS = 8
HEAD_DIM = 128
W = 512
BAND = 512
CB = 256


NEG_FILL = -1e30


def passed_along(array, axis, by):
    length = lax.axis_size(axis)
    pairs = [(i, i + by) for i in range(length) if 0 <= i + by < length]
    return lax.ppermute(array, axis, pairs)


def with_halo(array, sides, width):
    for axis, dim in sides:
        size, length = (lax.axis_size(axis), array.shape[dim])
        up = [(i, (i + 1) % size) for i in range(size - 1)]
        down = [(j, i) for i, j in up]
        last = lax.slice_in_dim(array, length - width, length, axis=dim)
        first = lax.slice_in_dim(array, 0, width, axis=dim)
        before = lax.ppermute(last, axis, up)
        after = lax.ppermute(first, axis, down)
        array = jnp.concatenate([before, array, after], axis=dim)
    return array


def head_split(matrix):
    return matrix.reshape(matrix.shape[0], HEADS, HEAD_DIM)


def attend(queries, key_rows, value_rows, allowed, time_bias):
    scores = jnp.einsum(
        "qhd,khd->hqk",
        head_split(queries),
        head_split(key_rows),
        preferred_element_type=jnp.float32,
    ) * HEAD_DIM ** (-0.5)
    scores = jnp.where(allowed[None], scores + time_bias, NEG_FILL)
    largest = jnp.max(scores, axis=2, keepdims=True)
    exponent = jnp.exp(scores - largest)
    weights = (exponent / jnp.sum(exponent, axis=2, keepdims=True)).astype(jnp.bfloat16)
    blended = jnp.einsum(
        "hqk,khd->qhd", weights, head_split(value_rows), preferred_element_type=jnp.float32
    )
    return blended.reshape(queries.shape[0], -1)


def normalize(sem_stream, norm_gain):
    scaled = sem_stream * lax.rsqrt(
        jnp.mean(sem_stream * sem_stream, axis=1, keepdims=True) + 1e-05
    )
    return (scaled * norm_gain[None, :]).astype(jnp.bfloat16)


def contract_rows(left_side, weight_piece):
    return jnp.dot(left_side, weight_piece, preferred_element_type=jnp.float32)


def coarse_kernel(prm, slopes_ref, q_ref, k_ref, v_ref, o_ref, *, blocks, near_rows):
    n = pl.program_id(0)
    band_low = prm[2 * n]
    band_high = prm[2 * n + 1]
    stream_start = prm[2 * blocks]
    live_count = prm[2 * blocks + 1]
    base_row = prm[2 * blocks + 2]
    rows = n * CB + lax.broadcasted_iota(jnp.int32, (CB, 1), 0)
    timing = ((stream_start + rows) // 2).astype(jnp.float32) * (2.0 / 3.0)
    key_global = base_row + lax.broadcasted_iota(jnp.int32, (1, near_rows), 1)
    inside = (key_global >= band_low) & (key_global < band_high)
    distance = jnp.abs(timing - key_global.astype(jnp.float32))
    live_rows = rows < live_count
    for h in range(HEADS):
        cols = slice(h * HEAD_DIM, (h + 1) * HEAD_DIM)
        scores = lax.dot_general(
            q_ref[:, cols], k_ref[:, cols], (((1,), (1,)), ((), ())),
            preferred_element_type=jnp.float32,
        ) * HEAD_DIM ** (-0.5)
        time_bias = distance * (-slopes_ref[h] / BAND)
        scores = jnp.where(inside, scores + time_bias, NEG_FILL)
        largest = jnp.max(scores, axis=1, keepdims=True)
        exponent = jnp.exp(scores - largest)
        total = jnp.sum(exponent, axis=1, keepdims=True)
        weights = (exponent * (1.0 / total)).astype(jnp.bfloat16)
        blended = jnp.dot(weights, v_ref[:, cols], preferred_element_type=jnp.float32)
        o_ref[:, cols] = jnp.where(live_rows, blended, 0.0).astype(jnp.bfloat16)


def coarse_attention(coarse_queries, near_pair, params, slopes):
    slots, width = coarse_queries.shape
    blocks = slots // CB
    near_rows = near_pair.shape[1]
    kernel = functools.partial(coarse_kernel, blocks=blocks, near_rows=near_rows)
    grid_spec = pltpu.PrefetchScalarGridSpec(
        num_scalar_prefetch=1,
        grid=(blocks,),
        in_specs=[
            pl.BlockSpec(memory_space=pltpu.SMEM),
            pl.BlockSpec((CB, width), lambda n, prm: (n, 0)),
            pl.BlockSpec((None, near_rows, width), lambda n, prm: (0, 0, 0)),
            pl.BlockSpec((None, near_rows, width), lambda n, prm: (1, 0, 0)),
        ],
        out_specs=pl.BlockSpec((CB, width), lambda n, prm: (n, 0)),
    )
    return pl.pallas_call(
        kernel,
        grid_spec=grid_spec,
        out_shape=jax.ShapeDtypeStruct((slots, width), jnp.bfloat16),
        compiler_params=pltpu.CompilerParams(dimension_semantics=("arbitrary",)),
    )(params, slopes, coarse_queries, near_pair, near_pair)


def on_device(
    sem_queries,
    sem_keys,
    sem_values,
    sem_inputs,
    out_proj,
    norm_gain,
    key_proj,
    value_proj,
    slopes,
    coarse_queries,
    counts,
    band_bounds,
):
    rows_here = sem_queries.shape[0]
    device_index = lax.axis_index("ctx")
    ctx_size = lax.axis_size("ctx")
    full_out_proj = lax.all_gather(out_proj, "ctx", axis=0, tiled=True)
    every_count = lax.all_gather(counts, "ctx", axis=0, tiled=True)
    every_count, sem_queries = lax.optimization_barrier((every_count, sem_queries))
    cross_rows, cross_cols = key_proj.shape
    stacked_proj = jnp.stack([key_proj, value_proj])
    gathered_proj = lax.all_gather(stacked_proj, "ctx", axis=1, tiled=True)
    own_pair = jnp.stack([sem_keys, sem_values])
    reach_shards = (W - 1 + rows_here - 1) // rows_here
    earlier = []
    for distance in range(1, reach_shards + 1):
        earlier.insert(0, passed_along(own_pair, "ctx", distance))
    window_pair = jnp.concatenate(earlier + [own_pair], axis=1)
    query_pos = jnp.arange(rows_here, dtype=jnp.int32)
    key_pos = jnp.arange(window_pair.shape[1], dtype=jnp.int32)
    key_lag = query_pos[:, None] + reach_shards * rows_here - key_pos[None, :]
    key_global = device_index * rows_here - reach_shards * rows_here + key_pos
    allowed = (key_lag >= 0) & (key_lag < W) & (key_global[None, :] >= 0)
    sem_att = attend(sem_queries, window_pair[0], window_pair[1], allowed, 0.0).astype(jnp.bfloat16)
    projected = contract_rows(sem_att, full_out_proj)
    sem_stream = sem_inputs.astype(jnp.float32) + projected
    normed = normalize(sem_stream, norm_gain)
    key_sum = contract_rows(normed, gathered_proj[0])
    value_sum = contract_rows(normed, gathered_proj[1])
    cross_keys = key_sum.astype(jnp.bfloat16)
    cross_values = value_sum.astype(jnp.bfloat16)
    earlier_index = jnp.arange(ctx_size, dtype=jnp.int32) < device_index
    stream_start = jnp.sum(jnp.where(earlier_index, every_count, 0)).astype(jnp.int32)
    near_pair = with_halo(jnp.stack([cross_keys, cross_values]), (("ctx", 1),), rows_here)
    base_row = (device_index - 1) * rows_here
    params = jnp.concatenate(
        [band_bounds.reshape(-1).astype(jnp.int32),
         jnp.stack([stream_start, counts[0], base_row]).astype(jnp.int32)]
    )
    return coarse_attention(coarse_queries, near_pair, params, slopes)


def solution(mesh):
    return jax.shard_map(
        on_device,
        mesh=mesh,
        in_specs=(
            P(("groups", "ctx"), None),
            P(("groups", "ctx"), None),
            P(("groups", "ctx"), None),
            P(("groups", "ctx"), None),
            P("ctx", None),
            P(),
            P("ctx", None),
            P("ctx", None),
            P(),
            P(("groups", "ctx"), None),
            P(("groups", "ctx")),
            P(("groups", "ctx"), None),
        ),
        out_specs=P(("groups", "ctx"), None),
        check_vma=False,
    )
```

```python
import functools

import jax
import jax.numpy as jnp
from jax import lax
from jax.experimental import pallas as pl
from jax.experimental.pallas import tpu as pltpu
from jax.sharding import PartitionSpec as P

HEADS = 8
HEAD_DIM = 128
W = 512
BAND = 512
CB = 256


NEG_FILL = -1e30


def passed_along(array, axis, by):
    length = lax.axis_size(axis)
    pairs = [(i, i + by) for i in range(length) if 0 <= i + by < length]
    return lax.ppermute(array, axis, pairs)


def with_halo(array, sides, width):
    for axis, dim in sides:
        size, length = (lax.axis_size(axis), array.shape[dim])
        up = [(i, (i + 1) % size) for i in range(size - 1)]
        down = [(j, i) for i, j in up]
        last = lax.slice_in_dim(array, length - width, length, axis=dim)
        first = lax.slice_in_dim(array, 0, width, axis=dim)
        before = lax.ppermute(last, axis, up)
        after = lax.ppermute(first, axis, down)
        array = jnp.concatenate([before, array, after], axis=dim)
    return array


def head_split(matrix):
    return matrix.reshape(matrix.shape[0], HEADS, HEAD_DIM)


def attend(queries, key_rows, value_rows, allowed, time_bias):
    scores = jnp.einsum(
        "qhd,khd->hqk",
        head_split(queries),
        head_split(key_rows),
        preferred_element_type=jnp.float32,
    ) * HEAD_DIM ** (-0.5)
    scores = jnp.where(allowed[None], scores + time_bias, NEG_FILL)
    largest = jnp.max(scores, axis=2, keepdims=True)
    exponent = jnp.exp(scores - largest)
    weights = (exponent / jnp.sum(exponent, axis=2, keepdims=True)).astype(jnp.bfloat16)
    blended = jnp.einsum(
        "hqk,khd->qhd", weights, head_split(value_rows), preferred_element_type=jnp.float32
    )
    return blended.reshape(queries.shape[0], -1)


def normalize(sem_stream, norm_gain):
    scaled = sem_stream * lax.rsqrt(
        jnp.mean(sem_stream * sem_stream, axis=1, keepdims=True) + 1e-05
    )
    return (scaled * norm_gain[None, :]).astype(jnp.bfloat16)


def contract_rows(left_side, weight_piece):
    return jnp.dot(left_side, weight_piece, preferred_element_type=jnp.float32)


def coarse_kernel(prm, slopes_ref, q_ref, k_ref, v_ref, o_ref, *, blocks, near_rows):
    n = pl.program_id(0)
    band_low = prm[2 * n]
    band_high = prm[2 * n + 1]
    stream_start = prm[2 * blocks]
    live_count = prm[2 * blocks + 1]
    base_row = prm[2 * blocks + 2]
    rows = n * CB + lax.broadcasted_iota(jnp.int32, (CB, 1), 0)
    timing = ((stream_start + rows) // 2).astype(jnp.float32) * (2.0 / 3.0)
    key_global = base_row + lax.broadcasted_iota(jnp.int32, (1, near_rows), 1)
    inside = (key_global >= band_low) & (key_global < band_high)
    distance = jnp.abs(timing - key_global.astype(jnp.float32))
    live_rows = rows < live_count
    for h in range(HEADS):
        cols = slice(h * HEAD_DIM, (h + 1) * HEAD_DIM)
        scores = lax.dot_general(
            q_ref[:, cols], k_ref[:, cols], (((1,), (1,)), ((), ())),
            preferred_element_type=jnp.float32,
        ) * HEAD_DIM ** (-0.5)
        time_bias = distance * (-slopes_ref[h] / BAND)
        scores = jnp.where(inside, scores + time_bias, NEG_FILL)
        largest = jnp.max(scores, axis=1, keepdims=True)
        exponent = jnp.exp(scores - largest)
        total = jnp.sum(exponent, axis=1, keepdims=True)
        weights = (exponent * (1.0 / total)).astype(jnp.bfloat16)
        blended = jnp.dot(weights, v_ref[:, cols], preferred_element_type=jnp.float32)
        o_ref[:, cols] = jnp.where(live_rows, blended, 0.0).astype(jnp.bfloat16)


def coarse_attention(coarse_queries, near_pair, params, slopes):
    slots, width = coarse_queries.shape
    blocks = slots // CB
    near_rows = near_pair.shape[1]
    kernel = functools.partial(coarse_kernel, blocks=blocks, near_rows=near_rows)
    grid_spec = pltpu.PrefetchScalarGridSpec(
        num_scalar_prefetch=1,
        grid=(blocks,),
        in_specs=[
            pl.BlockSpec(memory_space=pltpu.SMEM),
            pl.BlockSpec((CB, width), lambda n, prm: (n, 0)),
            pl.BlockSpec((None, near_rows, width), lambda n, prm: (0, 0, 0)),
            pl.BlockSpec((None, near_rows, width), lambda n, prm: (1, 0, 0)),
        ],
        out_specs=pl.BlockSpec((CB, width), lambda n, prm: (n, 0)),
    )
    return pl.pallas_call(
        kernel,
        grid_spec=grid_spec,
        out_shape=jax.ShapeDtypeStruct((slots, width), jnp.bfloat16),
        compiler_params=pltpu.CompilerParams(dimension_semantics=("arbitrary",)),
    )(params, slopes, coarse_queries, near_pair, near_pair)


def on_device(
    sem_queries,
    sem_keys,
    sem_values,
    sem_inputs,
    out_proj,
    norm_gain,
    key_proj,
    value_proj,
    slopes,
    coarse_queries,
    counts,
    band_bounds,
):
    rows_here = sem_queries.shape[0]
    device_index = lax.axis_index("ctx")
    ctx_size = lax.axis_size("ctx")
    full_out_proj = lax.all_gather(out_proj, "ctx", axis=0, tiled=True)
    every_count = lax.all_gather(counts, "ctx", axis=0, tiled=True)
    every_count, sem_queries = lax.optimization_barrier((every_count, sem_queries))
    group_size = lax.axis_size("groups")
    shared = group_size % 2 == 0
    if shared:
        partners = [(i, i ^ 1) for i in range(group_size)]
        key_side = lax.axis_index("groups") % 2 == 0
        own_proj = jnp.where(key_side, key_proj, value_proj)
        gathered_proj = lax.all_gather(own_proj, "ctx", axis=0, tiled=True)
    else:
        stacked_proj = jnp.stack([key_proj, value_proj])
        gathered_proj = lax.all_gather(stacked_proj, "ctx", axis=1, tiled=True)
    own_pair = jnp.stack([sem_keys, sem_values])
    reach_shards = (W - 1 + rows_here - 1) // rows_here
    earlier = []
    for distance in range(1, reach_shards + 1):
        earlier.insert(0, passed_along(own_pair, "ctx", distance))
    window_pair = jnp.concatenate(earlier + [own_pair], axis=1)
    query_pos = jnp.arange(rows_here, dtype=jnp.int32)
    key_pos = jnp.arange(window_pair.shape[1], dtype=jnp.int32)
    key_lag = query_pos[:, None] + reach_shards * rows_here - key_pos[None, :]
    key_global = device_index * rows_here - reach_shards * rows_here + key_pos
    allowed = (key_lag >= 0) & (key_lag < W) & (key_global[None, :] >= 0)
    sem_att = attend(sem_queries, window_pair[0], window_pair[1], allowed, 0.0).astype(jnp.bfloat16)
    projected = contract_rows(sem_att, full_out_proj)
    sem_stream = sem_inputs.astype(jnp.float32) + projected
    normed = normalize(sem_stream, norm_gain)
    if shared:
        partner_normed = lax.ppermute(normed, "groups", partners)
        both_streams = jnp.concatenate([normed, partner_normed], axis=0)
        both_sums = contract_rows(both_streams, gathered_proj).astype(jnp.bfloat16)
        own_sum = both_sums[:rows_here]
        partner_sum = lax.ppermute(both_sums[rows_here:], "groups", partners)
        cross_keys = jnp.where(key_side, own_sum, partner_sum)
        cross_values = jnp.where(key_side, partner_sum, own_sum)
    else:
        cross_keys = contract_rows(normed, gathered_proj[0]).astype(jnp.bfloat16)
        cross_values = contract_rows(normed, gathered_proj[1]).astype(jnp.bfloat16)
    earlier_index = jnp.arange(ctx_size, dtype=jnp.int32) < device_index
    stream_start = jnp.sum(jnp.where(earlier_index, every_count, 0)).astype(jnp.int32)
    near_pair = with_halo(jnp.stack([cross_keys, cross_values]), (("ctx", 1),), rows_here)
    base_row = (device_index - 1) * rows_here
    params = jnp.concatenate(
        [band_bounds.reshape(-1).astype(jnp.int32),
         jnp.stack([stream_start, counts[0], base_row]).astype(jnp.int32)]
    )
    return coarse_attention(coarse_queries, near_pair, params, slopes)


def solution(mesh):
    return jax.shard_map(
        on_device,
        mesh=mesh,
        in_specs=(
            P(("groups", "ctx"), None),
            P(("groups", "ctx"), None),
            P(("groups", "ctx"), None),
            P(("groups", "ctx"), None),
            P("ctx", None),
            P(),
            P("ctx", None),
            P("ctx", None),
            P(),
            P(("groups", "ctx"), None),
            P(("groups", "ctx")),
            P(("groups", "ctx"), None),
        ),
        out_specs=P(("groups", "ctx"), None),
        check_vma=False,
    )
```

```python
import functools

import jax
import jax.numpy as jnp
from jax import lax
from jax.experimental import pallas as pl
from jax.experimental.pallas import tpu as pltpu
from jax.sharding import PartitionSpec as P

HEADS = 8
HEAD_DIM = 128
W = 512
BAND = 512
CB = 256


NEG_FILL = -1e30


def passed_along(array, axis, by):
    length = lax.axis_size(axis)
    pairs = [(i, i + by) for i in range(length) if 0 <= i + by < length]
    return lax.ppermute(array, axis, pairs)


def with_halo(array, sides, width):
    for axis, dim in sides:
        size, length = (lax.axis_size(axis), array.shape[dim])
        up = [(i, (i + 1) % size) for i in range(size - 1)]
        down = [(j, i) for i, j in up]
        last = lax.slice_in_dim(array, length - width, length, axis=dim)
        first = lax.slice_in_dim(array, 0, width, axis=dim)
        before = lax.ppermute(last, axis, up)
        after = lax.ppermute(first, axis, down)
        array = jnp.concatenate([before, array, after], axis=dim)
    return array


def head_split(matrix):
    return matrix.reshape(matrix.shape[0], HEADS, HEAD_DIM)


def attend(queries, key_rows, value_rows, allowed, time_bias):
    scores = jnp.einsum(
        "qhd,khd->hqk",
        head_split(queries),
        head_split(key_rows),
        preferred_element_type=jnp.float32,
    ) * HEAD_DIM ** (-0.5)
    scores = jnp.where(allowed[None], scores + time_bias, NEG_FILL)
    largest = jnp.max(scores, axis=2, keepdims=True)
    exponent = jnp.exp(scores - largest)
    weights = (exponent / jnp.sum(exponent, axis=2, keepdims=True)).astype(jnp.bfloat16)
    blended = jnp.einsum(
        "hqk,khd->qhd", weights, head_split(value_rows), preferred_element_type=jnp.float32
    )
    return blended.reshape(queries.shape[0], -1)


def normalize(sem_stream, norm_gain):
    scaled = sem_stream * lax.rsqrt(
        jnp.mean(sem_stream * sem_stream, axis=1, keepdims=True) + 1e-05
    )
    return (scaled * norm_gain[None, :]).astype(jnp.bfloat16)


def contract_rows(left_side, weight_piece):
    return jnp.dot(left_side, weight_piece, preferred_element_type=jnp.float32)


def coarse_kernel(prm, slopes_ref, q_ref, k_ref, v_ref, o_ref, *, blocks, near_rows):
    n = pl.program_id(0)
    band_low = prm[2 * n]
    band_high = prm[2 * n + 1]
    stream_start = prm[2 * blocks]
    live_count = prm[2 * blocks + 1]
    base_row = prm[2 * blocks + 2]
    rows = n * CB + lax.broadcasted_iota(jnp.int32, (CB, 1), 0)
    timing = ((stream_start + rows) // 2).astype(jnp.float32) * (2.0 / 3.0)
    key_global = base_row + lax.broadcasted_iota(jnp.int32, (1, near_rows), 1)
    inside = (key_global >= band_low) & (key_global < band_high)
    distance = jnp.abs(timing - key_global.astype(jnp.float32))
    live_rows = rows < live_count
    for h in range(HEADS):
        cols = slice(h * HEAD_DIM, (h + 1) * HEAD_DIM)
        scores = lax.dot_general(
            q_ref[:, cols], k_ref[:, cols], (((1,), (1,)), ((), ())),
            preferred_element_type=jnp.float32,
        ) * HEAD_DIM ** (-0.5)
        time_bias = distance * (-slopes_ref[h] / BAND)
        scores = jnp.where(inside, scores + time_bias, NEG_FILL)
        largest = jnp.max(scores, axis=1, keepdims=True)
        exponent = jnp.exp(scores - largest)
        total = jnp.sum(exponent, axis=1, keepdims=True)
        weights = (exponent * (1.0 / total)).astype(jnp.bfloat16)
        blended = jnp.dot(weights, v_ref[:, cols], preferred_element_type=jnp.float32)
        o_ref[:, cols] = jnp.where(live_rows, blended, 0.0).astype(jnp.bfloat16)


def coarse_attention(coarse_queries, near_pair, params, slopes):
    slots, width = coarse_queries.shape
    blocks = slots // CB
    near_rows = near_pair.shape[1]
    kernel = functools.partial(coarse_kernel, blocks=blocks, near_rows=near_rows)
    grid_spec = pltpu.PrefetchScalarGridSpec(
        num_scalar_prefetch=1,
        grid=(blocks,),
        in_specs=[
            pl.BlockSpec(memory_space=pltpu.SMEM),
            pl.BlockSpec((CB, width), lambda n, prm: (n, 0)),
            pl.BlockSpec((None, near_rows, width), lambda n, prm: (0, 0, 0)),
            pl.BlockSpec((None, near_rows, width), lambda n, prm: (1, 0, 0)),
        ],
        out_specs=pl.BlockSpec((CB, width), lambda n, prm: (n, 0)),
    )
    return pl.pallas_call(
        kernel,
        grid_spec=grid_spec,
        out_shape=jax.ShapeDtypeStruct((slots, width), jnp.bfloat16),
        compiler_params=pltpu.CompilerParams(dimension_semantics=("arbitrary",)),
    )(params, slopes, coarse_queries, near_pair, near_pair)


def on_device(
    sem_queries,
    sem_keys,
    sem_values,
    sem_inputs,
    out_proj,
    norm_gain,
    key_proj,
    value_proj,
    slopes,
    coarse_queries,
    counts,
    band_bounds,
):
    rows_here = sem_queries.shape[0]
    device_index = lax.axis_index("ctx")
    ctx_size = lax.axis_size("ctx")
    full_out_proj = lax.all_gather(out_proj, "ctx", axis=0, tiled=True)
    running = counts
    reach = 1
    while reach < ctx_size:
        running = running + passed_along(running, "ctx", reach)
        reach *= 2
    group_size = lax.axis_size("groups")
    shared = group_size % 2 == 0
    if shared:
        partners = [(i, i ^ 1) for i in range(group_size)]
        key_side = lax.axis_index("groups") % 2 == 0
        own_proj = jnp.where(key_side, key_proj, value_proj)
        gathered_proj = lax.all_gather(own_proj, "ctx", axis=0, tiled=True)
    else:
        stacked_proj = jnp.stack([key_proj, value_proj])
        gathered_proj = lax.all_gather(stacked_proj, "ctx", axis=1, tiled=True)
    own_pair = jnp.stack([sem_keys, sem_values])
    reach_shards = (W - 1 + rows_here - 1) // rows_here
    earlier = []
    for distance in range(1, reach_shards + 1):
        earlier.insert(0, passed_along(own_pair, "ctx", distance))
    window_pair = jnp.concatenate(earlier + [own_pair], axis=1)
    query_pos = jnp.arange(rows_here, dtype=jnp.int32)
    key_pos = jnp.arange(window_pair.shape[1], dtype=jnp.int32)
    key_lag = query_pos[:, None] + reach_shards * rows_here - key_pos[None, :]
    key_global = device_index * rows_here - reach_shards * rows_here + key_pos
    allowed = (key_lag >= 0) & (key_lag < W) & (key_global[None, :] >= 0)
    sem_att = attend(sem_queries, window_pair[0], window_pair[1], allowed, 0.0).astype(jnp.bfloat16)
    projected = contract_rows(sem_att, full_out_proj)
    sem_stream = sem_inputs.astype(jnp.float32) + projected
    normed = normalize(sem_stream, norm_gain)
    if shared:
        partner_normed = lax.ppermute(normed, "groups", partners)
        both_streams = jnp.concatenate([normed, partner_normed], axis=0)
        both_sums = contract_rows(both_streams, gathered_proj).astype(jnp.bfloat16)
        own_sum = both_sums[:rows_here]
        partner_sum = lax.ppermute(both_sums[rows_here:], "groups", partners)
        cross_keys = jnp.where(key_side, own_sum, partner_sum)
        cross_values = jnp.where(key_side, partner_sum, own_sum)
    else:
        cross_keys = contract_rows(normed, gathered_proj[0]).astype(jnp.bfloat16)
        cross_values = contract_rows(normed, gathered_proj[1]).astype(jnp.bfloat16)
    stream_start = (running - counts)[0]
    near_pair = with_halo(jnp.stack([cross_keys, cross_values]), (("ctx", 1),), rows_here)
    base_row = (device_index - 1) * rows_here
    params = jnp.concatenate(
        [band_bounds.reshape(-1).astype(jnp.int32),
         jnp.stack([stream_start, counts[0], base_row]).astype(jnp.int32)]
    )
    return coarse_attention(coarse_queries, near_pair, params, slopes)


def solution(mesh):
    return jax.shard_map(
        on_device,
        mesh=mesh,
        in_specs=(
            P(("groups", "ctx"), None),
            P(("groups", "ctx"), None),
            P(("groups", "ctx"), None),
            P(("groups", "ctx"), None),
            P("ctx", None),
            P(),
            P("ctx", None),
            P("ctx", None),
            P(),
            P(("groups", "ctx"), None),
            P(("groups", "ctx")),
            P(("groups", "ctx"), None),
        ),
        out_specs=P(("groups", "ctx"), None),
        check_vma=False,
    )
```

```python
import functools

import jax
import jax.numpy as jnp
from jax import lax
from jax.experimental import pallas as pl
from jax.experimental.pallas import tpu as pltpu
from jax.sharding import PartitionSpec as P

HEADS = 8
HEAD_DIM = 128
W = 512
BAND = 512
CB = 256


NEG_FILL = -1e30


def passed_along(array, axis, by):
    length = lax.axis_size(axis)
    pairs = [(i, i + by) for i in range(length) if 0 <= i + by < length]
    return lax.ppermute(array, axis, pairs)


def with_halo(array, sides, width):
    for axis, dim in sides:
        size, length = (lax.axis_size(axis), array.shape[dim])
        up = [(i, (i + 1) % size) for i in range(size - 1)]
        down = [(j, i) for i, j in up]
        last = lax.slice_in_dim(array, length - width, length, axis=dim)
        first = lax.slice_in_dim(array, 0, width, axis=dim)
        before = lax.ppermute(last, axis, up)
        after = lax.ppermute(first, axis, down)
        array = jnp.concatenate([before, array, after], axis=dim)
    return array


def head_split(matrix):
    return matrix.reshape(matrix.shape[0], HEADS, HEAD_DIM)


def attend(queries, key_rows, value_rows, allowed, time_bias):
    scores = jnp.einsum(
        "qhd,khd->hqk",
        head_split(queries),
        head_split(key_rows),
        preferred_element_type=jnp.float32,
    ) * HEAD_DIM ** (-0.5)
    scores = jnp.where(allowed[None], scores + time_bias, NEG_FILL)
    largest = jnp.max(scores, axis=2, keepdims=True)
    exponent = jnp.exp(scores - largest)
    weights = (exponent / jnp.sum(exponent, axis=2, keepdims=True)).astype(jnp.bfloat16)
    blended = jnp.einsum(
        "hqk,khd->qhd", weights, head_split(value_rows), preferred_element_type=jnp.float32
    )
    return blended.reshape(queries.shape[0], -1)


def normalize(sem_stream, norm_gain):
    scaled = sem_stream * lax.rsqrt(
        jnp.mean(sem_stream * sem_stream, axis=1, keepdims=True) + 1e-05
    )
    return (scaled * norm_gain[None, :]).astype(jnp.bfloat16)


def contract_rows(left_side, weight_piece):
    return jnp.dot(left_side, weight_piece, preferred_element_type=jnp.float32)


def coarse_kernel(prm, slopes_ref, q_ref, k_ref, v_ref, o_ref, *, blocks, near_rows):
    n = pl.program_id(0)
    band_low = prm[2 * n]
    band_high = prm[2 * n + 1]
    stream_start = prm[2 * blocks]
    live_count = prm[2 * blocks + 1]
    base_row = prm[2 * blocks + 2]
    rows = n * CB + lax.broadcasted_iota(jnp.int32, (CB, 1), 0)
    timing = ((stream_start + rows) // 2).astype(jnp.float32) * (2.0 / 3.0)
    key_global = base_row + lax.broadcasted_iota(jnp.int32, (1, near_rows), 1)
    inside = (key_global >= band_low) & (key_global < band_high)
    distance = jnp.abs(timing - key_global.astype(jnp.float32))
    live_rows = rows < live_count
    for h in range(HEADS):
        cols = slice(h * HEAD_DIM, (h + 1) * HEAD_DIM)
        scores = lax.dot_general(
            q_ref[:, cols], k_ref[:, cols], (((1,), (1,)), ((), ())),
            preferred_element_type=jnp.float32,
        ) * HEAD_DIM ** (-0.5)
        time_bias = distance * (-slopes_ref[h] / BAND)
        scores = jnp.where(inside, scores + time_bias, NEG_FILL)
        largest = jnp.max(scores, axis=1, keepdims=True)
        exponent = jnp.exp(scores - largest)
        total = jnp.sum(exponent, axis=1, keepdims=True)
        weights = (exponent * (1.0 / total)).astype(jnp.bfloat16)
        blended = jnp.dot(weights, v_ref[:, cols], preferred_element_type=jnp.float32)
        o_ref[:, cols] = jnp.where(live_rows, blended, 0.0).astype(jnp.bfloat16)


def coarse_attention(coarse_queries, near_pair, params, slopes):
    slots, width = coarse_queries.shape
    blocks = slots // CB
    near_rows = near_pair.shape[1]
    kernel = functools.partial(coarse_kernel, blocks=blocks, near_rows=near_rows)
    grid_spec = pltpu.PrefetchScalarGridSpec(
        num_scalar_prefetch=1,
        grid=(blocks,),
        in_specs=[
            pl.BlockSpec(memory_space=pltpu.SMEM),
            pl.BlockSpec((CB, width), lambda n, prm: (n, 0)),
            pl.BlockSpec((None, near_rows, width), lambda n, prm: (0, 0, 0)),
            pl.BlockSpec((None, near_rows, width), lambda n, prm: (1, 0, 0)),
        ],
        out_specs=pl.BlockSpec((CB, width), lambda n, prm: (n, 0)),
    )
    return pl.pallas_call(
        kernel,
        grid_spec=grid_spec,
        out_shape=jax.ShapeDtypeStruct((slots, width), jnp.bfloat16),
        compiler_params=pltpu.CompilerParams(dimension_semantics=("arbitrary",)),
    )(params, slopes, coarse_queries, near_pair, near_pair)


def on_device(
    sem_queries,
    sem_keys,
    sem_values,
    sem_inputs,
    out_proj,
    norm_gain,
    key_proj,
    value_proj,
    slopes,
    coarse_queries,
    counts,
    band_bounds,
):
    rows_here = sem_queries.shape[0]
    device_index = lax.axis_index("ctx")
    ctx_size = lax.axis_size("ctx")
    full_out_proj = lax.all_gather(out_proj, "ctx", axis=0, tiled=True)
    running = counts
    reach = 1
    while reach < ctx_size:
        running = running + passed_along(running, "ctx", reach)
        reach *= 2
    group_size = lax.axis_size("groups")
    shared = group_size % 2 == 0
    if shared:
        partners = [(i, i ^ 1) for i in range(group_size)]
        key_side = lax.axis_index("groups") % 2 == 0
        own_proj = jnp.where(key_side, key_proj, value_proj)
        gathered_proj = lax.all_gather(own_proj, "ctx", axis=0, tiled=True)
    else:
        stacked_proj = jnp.stack([key_proj, value_proj])
        gathered_proj = lax.all_gather(stacked_proj, "ctx", axis=1, tiled=True)
    own_pair = jnp.stack([sem_keys, sem_values])
    reach_shards = (W - 1 + rows_here - 1) // rows_here
    earlier = []
    for distance in range(1, reach_shards + 1):
        earlier.insert(0, passed_along(own_pair, "ctx", distance))
    window_pair = jnp.concatenate(earlier + [own_pair], axis=1)
    query_pos = jnp.arange(rows_here, dtype=jnp.int32)
    key_pos = jnp.arange(window_pair.shape[1], dtype=jnp.int32)
    key_lag = query_pos[:, None] + reach_shards * rows_here - key_pos[None, :]
    key_global = device_index * rows_here - reach_shards * rows_here + key_pos
    allowed = (key_lag >= 0) & (key_lag < W) & (key_global[None, :] >= 0)
    sem_att = attend(sem_queries, window_pair[0], window_pair[1], allowed, 0.0).astype(jnp.bfloat16)
    running, sem_att = lax.optimization_barrier((running, sem_att))
    projected = contract_rows(sem_att, full_out_proj)
    sem_stream = sem_inputs.astype(jnp.float32) + projected
    normed = normalize(sem_stream, norm_gain)
    if shared:
        partner_normed = lax.ppermute(normed, "groups", partners)
        both_streams = jnp.concatenate([normed, partner_normed], axis=0)
        both_sums = contract_rows(both_streams, gathered_proj).astype(jnp.bfloat16)
        own_sum = both_sums[:rows_here]
        partner_sum = lax.ppermute(both_sums[rows_here:], "groups", partners)
        cross_keys = jnp.where(key_side, own_sum, partner_sum)
        cross_values = jnp.where(key_side, partner_sum, own_sum)
    else:
        cross_keys = contract_rows(normed, gathered_proj[0]).astype(jnp.bfloat16)
        cross_values = contract_rows(normed, gathered_proj[1]).astype(jnp.bfloat16)
    stream_start = (running - counts)[0]
    near_pair = with_halo(jnp.stack([cross_keys, cross_values]), (("ctx", 1),), rows_here)
    base_row = (device_index - 1) * rows_here
    params = jnp.concatenate(
        [band_bounds.reshape(-1).astype(jnp.int32),
         jnp.stack([stream_start, counts[0], base_row]).astype(jnp.int32)]
    )
    return coarse_attention(coarse_queries, near_pair, params, slopes)


def solution(mesh):
    return jax.shard_map(
        on_device,
        mesh=mesh,
        in_specs=(
            P(("groups", "ctx"), None),
            P(("groups", "ctx"), None),
            P(("groups", "ctx"), None),
            P(("groups", "ctx"), None),
            P("ctx", None),
            P(),
            P("ctx", None),
            P("ctx", None),
            P(),
            P(("groups", "ctx"), None),
            P(("groups", "ctx")),
            P(("groups", "ctx"), None),
        ),
        out_specs=P(("groups", "ctx"), None),
        check_vma=False,
    )
```

```python
import functools

import jax
import jax.numpy as jnp
from jax import lax
from jax.experimental import pallas as pl
from jax.experimental.pallas import tpu as pltpu
from jax.sharding import PartitionSpec as P

HEADS = 8
HEAD_DIM = 128
W = 512
BAND = 512
CB = 256


NEG_FILL = -1e30


def passed_along(array, axis, by):
    length = lax.axis_size(axis)
    pairs = [(i, i + by) for i in range(length) if 0 <= i + by < length]
    return lax.ppermute(array, axis, pairs)


def with_halo(array, sides, width):
    for axis, dim in sides:
        size, length = (lax.axis_size(axis), array.shape[dim])
        up = [(i, (i + 1) % size) for i in range(size - 1)]
        down = [(j, i) for i, j in up]
        last = lax.slice_in_dim(array, length - width, length, axis=dim)
        first = lax.slice_in_dim(array, 0, width, axis=dim)
        before = lax.ppermute(last, axis, up)
        after = lax.ppermute(first, axis, down)
        array = jnp.concatenate([before, array, after], axis=dim)
    return array


def sent_to(array, group_flip, ctx_step):
    groups, length = (lax.axis_size("groups"), lax.axis_size("ctx"))
    pairs = [
        (g * length + c, (g ^ group_flip) * length + c + ctx_step)
        for g in range(groups)
        for c in range(length)
        if 0 <= c + ctx_step < length
    ]
    return lax.ppermute(array, ("groups", "ctx"), pairs)


def head_split(matrix):
    return matrix.reshape(matrix.shape[0], HEADS, HEAD_DIM)


def attend(queries, key_rows, value_rows, allowed, time_bias):
    scores = jnp.einsum(
        "qhd,khd->hqk",
        head_split(queries),
        head_split(key_rows),
        preferred_element_type=jnp.float32,
    ) * HEAD_DIM ** (-0.5)
    scores = jnp.where(allowed[None], scores + time_bias, NEG_FILL)
    largest = jnp.max(scores, axis=2, keepdims=True)
    exponent = jnp.exp(scores - largest)
    weights = (exponent / jnp.sum(exponent, axis=2, keepdims=True)).astype(jnp.bfloat16)
    blended = jnp.einsum(
        "hqk,khd->qhd", weights, head_split(value_rows), preferred_element_type=jnp.float32
    )
    return blended.reshape(queries.shape[0], -1)


def normalize(sem_stream, norm_gain):
    scaled = sem_stream * lax.rsqrt(
        jnp.mean(sem_stream * sem_stream, axis=1, keepdims=True) + 1e-05
    )
    return (scaled * norm_gain[None, :]).astype(jnp.bfloat16)


def contract_rows(left_side, weight_piece):
    return jnp.dot(left_side, weight_piece, preferred_element_type=jnp.float32)


def coarse_kernel(prm, slopes_ref, q_ref, k_ref, v_ref, o_ref, *, blocks, near_rows):
    n = pl.program_id(0)
    band_low = prm[2 * n]
    band_high = prm[2 * n + 1]
    stream_start = prm[2 * blocks]
    live_count = prm[2 * blocks + 1]
    base_row = prm[2 * blocks + 2]
    rows = n * CB + lax.broadcasted_iota(jnp.int32, (CB, 1), 0)
    timing = ((stream_start + rows) // 2).astype(jnp.float32) * (2.0 / 3.0)
    key_global = base_row + lax.broadcasted_iota(jnp.int32, (1, near_rows), 1)
    inside = (key_global >= band_low) & (key_global < band_high)
    distance = jnp.abs(timing - key_global.astype(jnp.float32))
    live_rows = rows < live_count
    for h in range(HEADS):
        cols = slice(h * HEAD_DIM, (h + 1) * HEAD_DIM)
        scores = lax.dot_general(
            q_ref[:, cols], k_ref[:, cols], (((1,), (1,)), ((), ())),
            preferred_element_type=jnp.float32,
        ) * HEAD_DIM ** (-0.5)
        time_bias = distance * (-slopes_ref[h] / BAND)
        scores = jnp.where(inside, scores + time_bias, NEG_FILL)
        largest = jnp.max(scores, axis=1, keepdims=True)
        exponent = jnp.exp(scores - largest)
        total = jnp.sum(exponent, axis=1, keepdims=True)
        weights = (exponent * (1.0 / total)).astype(jnp.bfloat16)
        blended = jnp.dot(weights, v_ref[:, cols], preferred_element_type=jnp.float32)
        o_ref[:, cols] = jnp.where(live_rows, blended, 0.0).astype(jnp.bfloat16)


def coarse_attention(coarse_queries, near_pair, params, slopes):
    slots, width = coarse_queries.shape
    blocks = slots // CB
    near_rows = near_pair.shape[1]
    kernel = functools.partial(coarse_kernel, blocks=blocks, near_rows=near_rows)
    grid_spec = pltpu.PrefetchScalarGridSpec(
        num_scalar_prefetch=1,
        grid=(blocks,),
        in_specs=[
            pl.BlockSpec(memory_space=pltpu.SMEM),
            pl.BlockSpec((CB, width), lambda n, prm: (n, 0)),
            pl.BlockSpec((None, near_rows, width), lambda n, prm: (prm[2 * blocks + 3], 0, 0)),
            pl.BlockSpec((None, near_rows, width), lambda n, prm: (1 - prm[2 * blocks + 3], 0, 0)),
        ],
        out_specs=pl.BlockSpec((CB, width), lambda n, prm: (n, 0)),
    )
    return pl.pallas_call(
        kernel,
        grid_spec=grid_spec,
        out_shape=jax.ShapeDtypeStruct((slots, width), jnp.bfloat16),
        compiler_params=pltpu.CompilerParams(dimension_semantics=("arbitrary",)),
    )(params, slopes, coarse_queries, near_pair, near_pair)


def on_device(
    sem_queries,
    sem_keys,
    sem_values,
    sem_inputs,
    out_proj,
    norm_gain,
    key_proj,
    value_proj,
    slopes,
    coarse_queries,
    counts,
    band_bounds,
):
    rows_here = sem_queries.shape[0]
    device_index = lax.axis_index("ctx")
    ctx_size = lax.axis_size("ctx")
    full_out_proj = lax.all_gather(out_proj, "ctx", axis=0, tiled=True)
    running = counts
    reach = 1
    while reach < ctx_size:
        running = running + passed_along(running, "ctx", reach)
        reach *= 2
    group_size = lax.axis_size("groups")
    shared = group_size % 2 == 0
    if shared:
        partners = [(i, i ^ 1) for i in range(group_size)]
        key_side = lax.axis_index("groups") % 2 == 0
        own_proj = jnp.where(key_side, key_proj, value_proj)
        gathered_proj = lax.all_gather(own_proj, "ctx", axis=0, tiled=True)
    else:
        stacked_proj = jnp.stack([key_proj, value_proj])
        gathered_proj = lax.all_gather(stacked_proj, "ctx", axis=1, tiled=True)
    own_pair = jnp.stack([sem_keys, sem_values])
    reach_shards = (W - 1 + rows_here - 1) // rows_here
    earlier = []
    for distance in range(1, reach_shards + 1):
        earlier.insert(0, passed_along(own_pair, "ctx", distance))
    window_pair = jnp.concatenate(earlier + [own_pair], axis=1)
    query_pos = jnp.arange(rows_here, dtype=jnp.int32)
    key_pos = jnp.arange(window_pair.shape[1], dtype=jnp.int32)
    key_lag = query_pos[:, None] + reach_shards * rows_here - key_pos[None, :]
    key_global = device_index * rows_here - reach_shards * rows_here + key_pos
    allowed = (key_lag >= 0) & (key_lag < W) & (key_global[None, :] >= 0)
    sem_att = attend(sem_queries, window_pair[0], window_pair[1], allowed, 0.0).astype(jnp.bfloat16)
    running, sem_att = lax.optimization_barrier((running, sem_att))
    projected = contract_rows(sem_att, full_out_proj)
    sem_stream = sem_inputs.astype(jnp.float32) + projected
    normed = normalize(sem_stream, norm_gain)
    if shared:
        partner_normed = lax.ppermute(normed, "groups", partners)
        both_streams = jnp.concatenate([normed, partner_normed], axis=0)
        both_sums = contract_rows(both_streams, gathered_proj).astype(jnp.bfloat16)
        own_sum = both_sums[:rows_here]
        partner_part = both_sums[rows_here:]
        mine_near = jnp.concatenate(
            [sent_to(own_sum, 0, 1), own_sum, sent_to(own_sum, 0, -1)], axis=0)
        other_near = jnp.concatenate(
            [sent_to(partner_part, 1, 1), sent_to(partner_part, 1, 0), sent_to(partner_part, 1, -1)], axis=0)
        near_pair = jnp.stack([mine_near, other_near])
        key_slot = jnp.where(key_side, 0, 1)
    else:
        cross_keys = contract_rows(normed, gathered_proj[0]).astype(jnp.bfloat16)
        cross_values = contract_rows(normed, gathered_proj[1]).astype(jnp.bfloat16)
        near_pair = with_halo(jnp.stack([cross_keys, cross_values]), (("ctx", 1),), rows_here)
        key_slot = jnp.zeros((), jnp.int32)
    stream_start = (running - counts)[0]
    base_row = (device_index - 1) * rows_here
    params = jnp.concatenate(
        [band_bounds.reshape(-1).astype(jnp.int32),
         jnp.stack([stream_start, counts[0], base_row, key_slot]).astype(jnp.int32)]
    )
    return coarse_attention(coarse_queries, near_pair, params, slopes)


def solution(mesh):
    return jax.shard_map(
        on_device,
        mesh=mesh,
        in_specs=(
            P(("groups", "ctx"), None),
            P(("groups", "ctx"), None),
            P(("groups", "ctx"), None),
            P(("groups", "ctx"), None),
            P("ctx", None),
            P(),
            P("ctx", None),
            P("ctx", None),
            P(),
            P(("groups", "ctx"), None),
            P(("groups", "ctx")),
            P(("groups", "ctx"), None),
        ),
        out_specs=P(("groups", "ctx"), None),
        check_vma=False,
    )
```

```python
import functools

import jax
import jax.numpy as jnp
from jax import lax
from jax.experimental import pallas as pl
from jax.experimental.pallas import tpu as pltpu
from jax.sharding import PartitionSpec as P

HEADS = 8
HEAD_DIM = 128
W = 512
BAND = 512
CB = 256


NEG_FILL = -1e30


def passed_along(array, axis, by):
    length = lax.axis_size(axis)
    pairs = [(i, i + by) for i in range(length) if 0 <= i + by < length]
    return lax.ppermute(array, axis, pairs)


def with_halo(array, sides, width):
    for axis, dim in sides:
        size, length = (lax.axis_size(axis), array.shape[dim])
        up = [(i, (i + 1) % size) for i in range(size - 1)]
        down = [(j, i) for i, j in up]
        last = lax.slice_in_dim(array, length - width, length, axis=dim)
        first = lax.slice_in_dim(array, 0, width, axis=dim)
        before = lax.ppermute(last, axis, up)
        after = lax.ppermute(first, axis, down)
        array = jnp.concatenate([before, array, after], axis=dim)
    return array


def sent_to(array, group_flip, ctx_step):
    groups, length = (lax.axis_size("groups"), lax.axis_size("ctx"))
    pairs = [
        (g * length + c, (g ^ group_flip) * length + c + ctx_step)
        for g in range(groups)
        for c in range(length)
        if 0 <= c + ctx_step < length
    ]
    return lax.ppermute(array, ("groups", "ctx"), pairs)


def head_split(matrix):
    return matrix.reshape(matrix.shape[0], HEADS, HEAD_DIM)


def attend(queries, key_rows, value_rows, allowed, time_bias):
    scores = jnp.einsum(
        "qhd,khd->hqk",
        head_split(queries),
        head_split(key_rows),
        preferred_element_type=jnp.float32,
    ) * HEAD_DIM ** (-0.5)
    scores = jnp.where(allowed[None], scores + time_bias, NEG_FILL)
    largest = jnp.max(scores, axis=2, keepdims=True)
    exponent = jnp.exp(scores - largest)
    weights = (exponent / jnp.sum(exponent, axis=2, keepdims=True)).astype(jnp.bfloat16)
    blended = jnp.einsum(
        "hqk,khd->qhd", weights, head_split(value_rows), preferred_element_type=jnp.float32
    )
    return blended.reshape(queries.shape[0], -1)


def normalize(sem_stream, norm_gain):
    scaled = sem_stream * lax.rsqrt(
        jnp.mean(sem_stream * sem_stream, axis=1, keepdims=True) + 1e-05
    )
    return (scaled * norm_gain[None, :]).astype(jnp.bfloat16)


def contract_rows(left_side, weight_piece):
    return jnp.dot(left_side, weight_piece, preferred_element_type=jnp.float32)


def coarse_kernel(prm, slopes_ref, q_ref, k_ref, v_ref, o_ref, *, blocks, near_rows, span):
    n = pl.program_id(0)
    band_low = prm[2 * n]
    band_high = prm[2 * n + 1]
    stream_start = prm[2 * blocks]
    live_count = prm[2 * blocks + 1]
    base_row = prm[2 * blocks + 2]
    first_key = jnp.minimum(band_low - base_row, near_rows - BAND)
    step = span - BAND
    window = pl.multiple_of(jnp.clip(first_key // step * step, 0, near_rows - span), step)
    rows = n * CB + lax.broadcasted_iota(jnp.int32, (CB, 1), 0)
    timing = ((stream_start + rows) // 2).astype(jnp.float32) * (2.0 / 3.0)
    key_global = base_row + window + lax.broadcasted_iota(jnp.int32, (1, span), 1)
    inside = (key_global >= band_low) & (key_global < band_high)
    distance = jnp.where(inside, jnp.abs(timing - key_global.astype(jnp.float32)), -NEG_FILL)
    live_rows = rows < live_count
    for h in range(HEADS):
        cols = slice(h * HEAD_DIM, (h + 1) * HEAD_DIM)
        scores = lax.dot_general(
            q_ref[:, cols], k_ref[pl.ds(window, span), cols], (((1,), (1,)), ((), ())),
            preferred_element_type=jnp.float32,
        ) * HEAD_DIM ** (-0.5)
        scores = scores + distance * (-slopes_ref[h] / BAND)
        largest = jnp.max(scores, axis=1, keepdims=True)
        exponent = jnp.exp(scores - largest)
        total = jnp.sum(exponent, axis=1, keepdims=True)
        weights = (exponent * (1.0 / total)).astype(jnp.bfloat16)
        blended = jnp.dot(weights, v_ref[pl.ds(window, span), cols], preferred_element_type=jnp.float32)
        o_ref[:, cols] = jnp.where(live_rows, blended, 0.0).astype(jnp.bfloat16)


def coarse_attention(coarse_queries, near_pair, params, slopes):
    slots, width = coarse_queries.shape
    blocks = slots // CB
    near_rows = near_pair.shape[1]
    kernel = functools.partial(coarse_kernel, blocks=blocks, near_rows=near_rows, span=BAND + 128)
    grid_spec = pltpu.PrefetchScalarGridSpec(
        num_scalar_prefetch=1,
        grid=(blocks,),
        in_specs=[
            pl.BlockSpec(memory_space=pltpu.SMEM),
            pl.BlockSpec((CB, width), lambda n, prm: (n, 0)),
            pl.BlockSpec((None, near_rows, width), lambda n, prm: (prm[2 * blocks + 3], 0, 0)),
            pl.BlockSpec((None, near_rows, width), lambda n, prm: (1 - prm[2 * blocks + 3], 0, 0)),
        ],
        out_specs=pl.BlockSpec((CB, width), lambda n, prm: (n, 0)),
    )
    return pl.pallas_call(
        kernel,
        grid_spec=grid_spec,
        out_shape=jax.ShapeDtypeStruct((slots, width), jnp.bfloat16),
        compiler_params=pltpu.CompilerParams(dimension_semantics=("arbitrary",)),
    )(params, slopes, coarse_queries, near_pair, near_pair)


def on_device(
    sem_queries,
    sem_keys,
    sem_values,
    sem_inputs,
    out_proj,
    norm_gain,
    key_proj,
    value_proj,
    slopes,
    coarse_queries,
    counts,
    band_bounds,
):
    rows_here = sem_queries.shape[0]
    device_index = lax.axis_index("ctx")
    ctx_size = lax.axis_size("ctx")
    full_out_proj = lax.all_gather(out_proj, "ctx", axis=0, tiled=True)
    running = counts
    reach = 1
    while reach < ctx_size:
        running = running + passed_along(running, "ctx", reach)
        reach *= 2
    group_size = lax.axis_size("groups")
    shared = group_size % 2 == 0
    if shared:
        partners = [(i, i ^ 1) for i in range(group_size)]
        key_side = lax.axis_index("groups") % 2 == 0
        own_proj = jnp.where(key_side, key_proj, value_proj)
        gathered_proj = lax.all_gather(own_proj, "ctx", axis=0, tiled=True)
    else:
        stacked_proj = jnp.stack([key_proj, value_proj])
        gathered_proj = lax.all_gather(stacked_proj, "ctx", axis=1, tiled=True)
    own_pair = jnp.stack([sem_keys, sem_values])
    reach_shards = (W - 1 + rows_here - 1) // rows_here
    earlier = []
    for distance in range(1, reach_shards + 1):
        earlier.insert(0, passed_along(own_pair, "ctx", distance))
    window_pair = jnp.concatenate(earlier + [own_pair], axis=1)
    query_pos = jnp.arange(rows_here, dtype=jnp.int32)
    key_pos = jnp.arange(window_pair.shape[1], dtype=jnp.int32)
    key_lag = query_pos[:, None] + reach_shards * rows_here - key_pos[None, :]
    key_global = device_index * rows_here - reach_shards * rows_here + key_pos
    allowed = (key_lag >= 0) & (key_lag < W) & (key_global[None, :] >= 0)
    sem_att = attend(sem_queries, window_pair[0], window_pair[1], allowed, 0.0).astype(jnp.bfloat16)
    running, sem_att = lax.optimization_barrier((running, sem_att))
    projected = contract_rows(sem_att, full_out_proj)
    sem_stream = sem_inputs.astype(jnp.float32) + projected
    normed = normalize(sem_stream, norm_gain)
    if shared:
        partner_normed = lax.ppermute(normed, "groups", partners)
        both_streams = jnp.concatenate([normed, partner_normed], axis=0)
        both_sums = contract_rows(both_streams, gathered_proj).astype(jnp.bfloat16)
        own_sum = both_sums[:rows_here]
        partner_part = both_sums[rows_here:]
        mine_near = jnp.concatenate(
            [sent_to(own_sum, 0, 1), own_sum, sent_to(own_sum, 0, -1)], axis=0)
        other_near = jnp.concatenate(
            [sent_to(partner_part, 1, 1), sent_to(partner_part, 1, 0), sent_to(partner_part, 1, -1)], axis=0)
        near_pair = jnp.stack([mine_near, other_near])
        key_slot = jnp.where(key_side, 0, 1)
    else:
        cross_keys = contract_rows(normed, gathered_proj[0]).astype(jnp.bfloat16)
        cross_values = contract_rows(normed, gathered_proj[1]).astype(jnp.bfloat16)
        near_pair = with_halo(jnp.stack([cross_keys, cross_values]), (("ctx", 1),), rows_here)
        key_slot = jnp.zeros((), jnp.int32)
    stream_start = (running - counts)[0]
    base_row = (device_index - 1) * rows_here
    params = jnp.concatenate(
        [band_bounds.reshape(-1).astype(jnp.int32),
         jnp.stack([stream_start, counts[0], base_row, key_slot]).astype(jnp.int32)]
    )
    return coarse_attention(coarse_queries, near_pair, params, slopes)


def solution(mesh):
    return jax.shard_map(
        on_device,
        mesh=mesh,
        in_specs=(
            P(("groups", "ctx"), None),
            P(("groups", "ctx"), None),
            P(("groups", "ctx"), None),
            P(("groups", "ctx"), None),
            P("ctx", None),
            P(),
            P("ctx", None),
            P("ctx", None),
            P(),
            P(("groups", "ctx"), None),
            P(("groups", "ctx")),
            P(("groups", "ctx"), None),
        ),
        out_specs=P(("groups", "ctx"), None),
        check_vma=False,
    )
```

```python
import functools

import jax
import jax.numpy as jnp
from jax import lax
from jax.experimental import pallas as pl
from jax.experimental.pallas import tpu as pltpu
from jax.sharding import PartitionSpec as P

HEADS = 8
HEAD_DIM = 128
W = 512
BAND = 512
CB = 256


NEG_FILL = -1e30


def passed_along(array, axis, by):
    length = lax.axis_size(axis)
    pairs = [(i, i + by) for i in range(length) if 0 <= i + by < length]
    return lax.ppermute(array, axis, pairs)


def with_halo(array, sides, width):
    for axis, dim in sides:
        size, length = (lax.axis_size(axis), array.shape[dim])
        up = [(i, (i + 1) % size) for i in range(size - 1)]
        down = [(j, i) for i, j in up]
        last = lax.slice_in_dim(array, length - width, length, axis=dim)
        first = lax.slice_in_dim(array, 0, width, axis=dim)
        before = lax.ppermute(last, axis, up)
        after = lax.ppermute(first, axis, down)
        array = jnp.concatenate([before, array, after], axis=dim)
    return array


def sent_to(array, group_flip, ctx_step):
    groups, length = (lax.axis_size("groups"), lax.axis_size("ctx"))
    pairs = [
        (g * length + c, (g ^ group_flip) * length + c + ctx_step)
        for g in range(groups)
        for c in range(length)
        if 0 <= c + ctx_step < length
    ]
    return lax.ppermute(array, ("groups", "ctx"), pairs)


def head_split(matrix):
    return matrix.reshape(matrix.shape[0], HEADS, HEAD_DIM)


def attend(queries, key_rows, value_rows, allowed, time_bias):
    scores = jnp.einsum(
        "qhd,khd->hqk",
        head_split(queries),
        head_split(key_rows),
        preferred_element_type=jnp.float32,
    ) * HEAD_DIM ** (-0.5)
    scores = jnp.where(allowed[None], scores + time_bias, NEG_FILL)
    largest = jnp.max(scores, axis=2, keepdims=True)
    exponent = jnp.exp(scores - largest)
    weights = (exponent / jnp.sum(exponent, axis=2, keepdims=True)).astype(jnp.bfloat16)
    blended = jnp.einsum(
        "hqk,khd->qhd", weights, head_split(value_rows), preferred_element_type=jnp.float32
    )
    return blended.reshape(queries.shape[0], -1)


def normalize(sem_stream, norm_gain):
    scaled = sem_stream * lax.rsqrt(
        jnp.mean(sem_stream * sem_stream, axis=1, keepdims=True) + 1e-05
    )
    return (scaled * norm_gain[None, :]).astype(jnp.bfloat16)


def contract_rows(left_side, weight_piece):
    return jnp.dot(left_side, weight_piece, preferred_element_type=jnp.float32)


def coarse_kernel(prm, slopes_ref, q_ref, k_ref, v_ref, o_ref, *, blocks, near_rows, span, first_head, heads):
    n = pl.program_id(0)
    band_low = prm[2 * n]
    band_high = prm[2 * n + 1]
    stream_start = prm[2 * blocks]
    live_count = prm[2 * blocks + 1]
    base_row = prm[2 * blocks + 2]
    first_key = jnp.minimum(band_low - base_row, near_rows - BAND)
    step = span - BAND
    window = pl.multiple_of(jnp.clip(first_key // step * step, 0, near_rows - span), step)
    rows = n * CB + lax.broadcasted_iota(jnp.int32, (CB, 1), 0)
    timing = ((stream_start + rows) // 2).astype(jnp.float32) * (2.0 / 3.0)
    key_global = base_row + window + lax.broadcasted_iota(jnp.int32, (1, span), 1)
    inside = (key_global >= band_low) & (key_global < band_high)
    distance = jnp.where(inside, jnp.abs(timing - key_global.astype(jnp.float32)), -NEG_FILL)
    live_rows = rows < live_count
    for h in range(heads):
        cols = slice(h * HEAD_DIM, (h + 1) * HEAD_DIM)
        scores = lax.dot_general(
            q_ref[:, cols], k_ref[pl.ds(window, span), cols], (((1,), (1,)), ((), ())),
            preferred_element_type=jnp.float32,
        ) * HEAD_DIM ** (-0.5)
        scores = scores + distance * (-slopes_ref[first_head + h] / BAND)
        largest = jnp.max(scores, axis=1, keepdims=True)
        exponent = jnp.exp(scores - largest)
        total = jnp.sum(exponent, axis=1, keepdims=True)
        weights = (exponent * (1.0 / total)).astype(jnp.bfloat16)
        blended = jnp.dot(weights, v_ref[pl.ds(window, span), cols], preferred_element_type=jnp.float32)
        o_ref[:, cols] = jnp.where(live_rows, blended, 0.0).astype(jnp.bfloat16)


def coarse_attention(coarse_queries, near_pair, params, slopes, first_head, heads):
    slots = coarse_queries.shape[0]
    blocks = slots // CB
    near_rows, width = near_pair.shape[1:]
    kernel = functools.partial(
        coarse_kernel, blocks=blocks, near_rows=near_rows, span=BAND + 128,
        first_head=first_head, heads=heads,
    )
    column_block = first_head // heads
    grid_spec = pltpu.PrefetchScalarGridSpec(
        num_scalar_prefetch=1,
        grid=(blocks,),
        in_specs=[
            pl.BlockSpec(memory_space=pltpu.SMEM),
            pl.BlockSpec((CB, width), lambda n, prm: (n, column_block)),
            pl.BlockSpec((None, near_rows, width), lambda n, prm: (prm[2 * blocks + 3], 0, 0)),
            pl.BlockSpec((None, near_rows, width), lambda n, prm: (1 - prm[2 * blocks + 3], 0, 0)),
        ],
        out_specs=pl.BlockSpec((CB, width), lambda n, prm: (n, 0)),
    )
    return pl.pallas_call(
        kernel,
        grid_spec=grid_spec,
        out_shape=jax.ShapeDtypeStruct((slots, width), jnp.bfloat16),
        compiler_params=pltpu.CompilerParams(dimension_semantics=("arbitrary",)),
    )(params, slopes, coarse_queries, near_pair, near_pair)


def on_device(
    sem_queries,
    sem_keys,
    sem_values,
    sem_inputs,
    out_proj,
    norm_gain,
    key_proj,
    value_proj,
    slopes,
    coarse_queries,
    counts,
    band_bounds,
):
    rows_here = sem_queries.shape[0]
    device_index = lax.axis_index("ctx")
    ctx_size = lax.axis_size("ctx")
    full_out_proj = lax.all_gather(out_proj, "ctx", axis=0, tiled=True)
    running = counts
    reach = 1
    while reach < ctx_size:
        running = running + passed_along(running, "ctx", reach)
        reach *= 2
    group_size = lax.axis_size("groups")
    shared = group_size % 2 == 0
    if shared:
        partners = [(i, i ^ 1) for i in range(group_size)]
        key_side = lax.axis_index("groups") % 2 == 0
        own_proj = jnp.where(key_side, key_proj, value_proj)
        gathered_proj = lax.all_gather(own_proj, "ctx", axis=0, tiled=True)
    else:
        stacked_proj = jnp.stack([key_proj, value_proj])
        gathered_proj = lax.all_gather(stacked_proj, "ctx", axis=1, tiled=True)
    own_pair = jnp.stack([sem_keys, sem_values])
    reach_shards = (W - 1 + rows_here - 1) // rows_here
    earlier = []
    for distance in range(1, reach_shards + 1):
        earlier.insert(0, passed_along(own_pair, "ctx", distance))
    window_pair = jnp.concatenate(earlier + [own_pair], axis=1)
    query_pos = jnp.arange(rows_here, dtype=jnp.int32)
    key_pos = jnp.arange(window_pair.shape[1], dtype=jnp.int32)
    key_lag = query_pos[:, None] + reach_shards * rows_here - key_pos[None, :]
    key_global = device_index * rows_here - reach_shards * rows_here + key_pos
    allowed = (key_lag >= 0) & (key_lag < W) & (key_global[None, :] >= 0)
    sem_att = attend(sem_queries, window_pair[0], window_pair[1], allowed, 0.0).astype(jnp.bfloat16)
    running, sem_att = lax.optimization_barrier((running, sem_att))
    projected = contract_rows(sem_att, full_out_proj)
    sem_stream = sem_inputs.astype(jnp.float32) + projected
    normed = normalize(sem_stream, norm_gain)
    if shared:
        partner_normed = lax.ppermute(normed, "groups", partners)
        both_streams = jnp.concatenate([normed, partner_normed], axis=0)
        both_sums = contract_rows(both_streams, gathered_proj).astype(jnp.bfloat16)
        pieces = []
        half = both_sums.shape[1] // 2
        for part in range(2):
            piece = both_sums[:, part * half:(part + 1) * half]
            if pieces:
                _, piece = lax.optimization_barrier((pieces[-1], piece))
            own_sum = piece[:rows_here]
            partner_part = piece[rows_here:]
            mine_near = jnp.concatenate(
                [sent_to(own_sum, 0, 1), own_sum, sent_to(own_sum, 0, -1)], axis=0)
            other_near = jnp.concatenate(
                [sent_to(partner_part, 1, 1), sent_to(partner_part, 1, 0), sent_to(partner_part, 1, -1)], axis=0)
            pieces.append(jnp.stack([mine_near, other_near]))
        key_slot = jnp.where(key_side, 0, 1)
    else:
        cross_keys = contract_rows(normed, gathered_proj[0]).astype(jnp.bfloat16)
        cross_values = contract_rows(normed, gathered_proj[1]).astype(jnp.bfloat16)
        pieces = [with_halo(jnp.stack([cross_keys, cross_values]), (("ctx", 1),), rows_here)]
        key_slot = jnp.zeros((), jnp.int32)
    stream_start = (running - counts)[0]
    base_row = (device_index - 1) * rows_here
    params = jnp.concatenate(
        [band_bounds.reshape(-1).astype(jnp.int32),
         jnp.stack([stream_start, counts[0], base_row, key_slot]).astype(jnp.int32)]
    )
    heads = HEADS // len(pieces)
    outputs = [
        coarse_attention(coarse_queries, piece, params, slopes, part * heads, heads)
        for part, piece in enumerate(pieces)
    ]
    return jnp.concatenate(outputs, axis=1)


def solution(mesh):
    return jax.shard_map(
        on_device,
        mesh=mesh,
        in_specs=(
            P(("groups", "ctx"), None),
            P(("groups", "ctx"), None),
            P(("groups", "ctx"), None),
            P(("groups", "ctx"), None),
            P("ctx", None),
            P(),
            P("ctx", None),
            P("ctx", None),
            P(),
            P(("groups", "ctx"), None),
            P(("groups", "ctx")),
            P(("groups", "ctx"), None),
        ),
        out_specs=P(("groups", "ctx"), None),
        check_vma=False,
    )
```

```python
import functools

import jax
import jax.numpy as jnp
from jax import lax
from jax.experimental import pallas as pl
from jax.experimental.pallas import tpu as pltpu
from jax.sharding import PartitionSpec as P

HEADS = 8
HEAD_DIM = 128
W = 512
BAND = 512
CB = 256


NEG_FILL = -1e30


def passed_along(array, axis, by):
    length = lax.axis_size(axis)
    pairs = [(i, i + by) for i in range(length) if 0 <= i + by < length]
    return lax.ppermute(array, axis, pairs)


def with_halo(array, sides, width):
    for axis, dim in sides:
        size, length = (lax.axis_size(axis), array.shape[dim])
        up = [(i, (i + 1) % size) for i in range(size - 1)]
        down = [(j, i) for i, j in up]
        last = lax.slice_in_dim(array, length - width, length, axis=dim)
        first = lax.slice_in_dim(array, 0, width, axis=dim)
        before = lax.ppermute(last, axis, up)
        after = lax.ppermute(first, axis, down)
        array = jnp.concatenate([before, array, after], axis=dim)
    return array


def sent_to(array, group_flip, ctx_step):
    groups, length = (lax.axis_size("groups"), lax.axis_size("ctx"))
    pairs = [
        (g * length + c, (g ^ group_flip) * length + c + ctx_step)
        for g in range(groups)
        for c in range(length)
        if 0 <= c + ctx_step < length
    ]
    return lax.ppermute(array, ("groups", "ctx"), pairs)


def head_split(matrix):
    return matrix.reshape(matrix.shape[0], HEADS, HEAD_DIM)


def attend(queries, key_rows, value_rows, allowed, time_bias):
    scores = jnp.einsum(
        "qhd,khd->hqk",
        head_split(queries),
        head_split(key_rows),
        preferred_element_type=jnp.float32,
    ) * HEAD_DIM ** (-0.5)
    scores = jnp.where(allowed[None], scores + time_bias, NEG_FILL)
    largest = jnp.max(scores, axis=2, keepdims=True)
    exponent = jnp.exp(scores - largest)
    weights = (exponent / jnp.sum(exponent, axis=2, keepdims=True)).astype(jnp.bfloat16)
    blended = jnp.einsum(
        "hqk,khd->qhd", weights, head_split(value_rows), preferred_element_type=jnp.float32
    )
    return blended.reshape(queries.shape[0], -1)


def normalize(sem_stream, norm_gain):
    scaled = sem_stream * lax.rsqrt(
        jnp.mean(sem_stream * sem_stream, axis=1, keepdims=True) + 1e-05
    )
    return (scaled * norm_gain[None, :]).astype(jnp.bfloat16)


def contract_rows(left_side, weight_piece):
    return jnp.dot(left_side, weight_piece, preferred_element_type=jnp.float32)


def coarse_kernel(prm, slopes_ref, q_ref, k_ref, v_ref, o_ref, *, blocks, near_rows, span):
    n = pl.program_id(0)
    band_low = prm[2 * n]
    band_high = prm[2 * n + 1]
    stream_start = prm[2 * blocks]
    live_count = prm[2 * blocks + 1]
    base_row = prm[2 * blocks + 2]
    first_key = jnp.minimum(band_low - base_row, near_rows - BAND)
    step = span - BAND
    window = pl.multiple_of(jnp.clip(first_key // step * step, 0, near_rows - span), step)
    rows = n * CB + lax.broadcasted_iota(jnp.int32, (1, CB), 1)
    timing = ((stream_start + rows) // 2).astype(jnp.float32) * (2.0 / 3.0)
    key_global = base_row + window + lax.broadcasted_iota(jnp.int32, (span, 1), 0)
    inside = (key_global >= band_low) & (key_global < band_high)
    distance = jnp.where(inside, jnp.abs(timing - key_global.astype(jnp.float32)), -NEG_FILL)
    live_rows = n * CB + lax.broadcasted_iota(jnp.int32, (CB, 1), 0) < live_count
    for h in range(HEADS):
        cols = slice(h * HEAD_DIM, (h + 1) * HEAD_DIM)
        scores = lax.dot_general(
            k_ref[pl.ds(window, span), cols], q_ref[:, cols], (((1,), (1,)), ((), ())),
            preferred_element_type=jnp.float32,
        ) * HEAD_DIM ** (-0.5)
        scores = scores + distance * (-slopes_ref[h] / BAND)
        largest = jnp.max(scores, axis=0, keepdims=True)
        exponent = jnp.exp(scores - largest)
        total = jnp.sum(exponent, axis=0, keepdims=True)
        weights = (exponent * (1.0 / total)).astype(jnp.bfloat16)
        blended = lax.dot_general(
            weights, v_ref[pl.ds(window, span), cols], (((0,), (0,)), ((), ())),
            preferred_element_type=jnp.float32,
        )
        o_ref[:, cols] = jnp.where(live_rows, blended, 0.0).astype(jnp.bfloat16)


def coarse_attention(coarse_queries, near_pair, params, slopes):
    slots, width = coarse_queries.shape
    blocks = slots // CB
    near_rows = near_pair.shape[1]
    kernel = functools.partial(coarse_kernel, blocks=blocks, near_rows=near_rows, span=BAND + 128)
    grid_spec = pltpu.PrefetchScalarGridSpec(
        num_scalar_prefetch=1,
        grid=(blocks,),
        in_specs=[
            pl.BlockSpec(memory_space=pltpu.SMEM),
            pl.BlockSpec((CB, width), lambda n, prm: (n, 0)),
            pl.BlockSpec((None, near_rows, width), lambda n, prm: (prm[2 * blocks + 3], 0, 0)),
            pl.BlockSpec((None, near_rows, width), lambda n, prm: (1 - prm[2 * blocks + 3], 0, 0)),
        ],
        out_specs=pl.BlockSpec((CB, width), lambda n, prm: (n, 0)),
    )
    return pl.pallas_call(
        kernel,
        grid_spec=grid_spec,
        out_shape=jax.ShapeDtypeStruct((slots, width), jnp.bfloat16),
        compiler_params=pltpu.CompilerParams(dimension_semantics=("arbitrary",)),
    )(params, slopes, coarse_queries, near_pair, near_pair)


def on_device(
    sem_queries,
    sem_keys,
    sem_values,
    sem_inputs,
    out_proj,
    norm_gain,
    key_proj,
    value_proj,
    slopes,
    coarse_queries,
    counts,
    band_bounds,
):
    rows_here = sem_queries.shape[0]
    device_index = lax.axis_index("ctx")
    ctx_size = lax.axis_size("ctx")
    full_out_proj = lax.all_gather(out_proj, "ctx", axis=0, tiled=True)
    running = counts
    reach = 1
    while reach < ctx_size:
        running = running + passed_along(running, "ctx", reach)
        reach *= 2
    group_size = lax.axis_size("groups")
    shared = group_size % 2 == 0
    if shared:
        partners = [(i, i ^ 1) for i in range(group_size)]
        key_side = lax.axis_index("groups") % 2 == 0
        own_proj = jnp.where(key_side, key_proj, value_proj)
        gathered_proj = lax.all_gather(own_proj, "ctx", axis=0, tiled=True)
    else:
        stacked_proj = jnp.stack([key_proj, value_proj])
        gathered_proj = lax.all_gather(stacked_proj, "ctx", axis=1, tiled=True)
    own_pair = jnp.stack([sem_keys, sem_values])
    reach_shards = (W - 1 + rows_here - 1) // rows_here
    earlier = []
    for distance in range(1, reach_shards + 1):
        earlier.insert(0, passed_along(own_pair, "ctx", distance))
    window_pair = jnp.concatenate(earlier + [own_pair], axis=1)
    query_pos = jnp.arange(rows_here, dtype=jnp.int32)
    key_pos = jnp.arange(window_pair.shape[1], dtype=jnp.int32)
    key_lag = query_pos[:, None] + reach_shards * rows_here - key_pos[None, :]
    key_global = device_index * rows_here - reach_shards * rows_here + key_pos
    allowed = (key_lag >= 0) & (key_lag < W) & (key_global[None, :] >= 0)
    sem_att = attend(sem_queries, window_pair[0], window_pair[1], allowed, 0.0).astype(jnp.bfloat16)
    running, sem_att = lax.optimization_barrier((running, sem_att))
    projected = contract_rows(sem_att, full_out_proj)
    sem_stream = sem_inputs.astype(jnp.float32) + projected
    normed = normalize(sem_stream, norm_gain)
    if shared:
        partner_normed = lax.ppermute(normed, "groups", partners)
        both_streams = jnp.concatenate([normed, partner_normed], axis=0)
        both_sums = contract_rows(both_streams, gathered_proj).astype(jnp.bfloat16)
        own_sum = both_sums[:rows_here]
        partner_part = both_sums[rows_here:]
        mine_near = jnp.concatenate(
            [sent_to(own_sum, 0, 1), own_sum, sent_to(own_sum, 0, -1)], axis=0)
        other_near = jnp.concatenate(
            [sent_to(partner_part, 1, 1), sent_to(partner_part, 1, 0), sent_to(partner_part, 1, -1)], axis=0)
        near_pair = jnp.stack([mine_near, other_near])
        key_slot = jnp.where(key_side, 0, 1)
    else:
        cross_keys = contract_rows(normed, gathered_proj[0]).astype(jnp.bfloat16)
        cross_values = contract_rows(normed, gathered_proj[1]).astype(jnp.bfloat16)
        near_pair = with_halo(jnp.stack([cross_keys, cross_values]), (("ctx", 1),), rows_here)
        key_slot = jnp.zeros((), jnp.int32)
    stream_start = (running - counts)[0]
    base_row = (device_index - 1) * rows_here
    params = jnp.concatenate(
        [band_bounds.reshape(-1).astype(jnp.int32),
         jnp.stack([stream_start, counts[0], base_row, key_slot]).astype(jnp.int32)]
    )
    return coarse_attention(coarse_queries, near_pair, params, slopes)


def solution(mesh):
    return jax.shard_map(
        on_device,
        mesh=mesh,
        in_specs=(
            P(("groups", "ctx"), None),
            P(("groups", "ctx"), None),
            P(("groups", "ctx"), None),
            P(("groups", "ctx"), None),
            P("ctx", None),
            P(),
            P("ctx", None),
            P("ctx", None),
            P(),
            P(("groups", "ctx"), None),
            P(("groups", "ctx")),
            P(("groups", "ctx"), None),
        ),
        out_specs=P(("groups", "ctx"), None),
        check_vma=False,
    )
```

```python
import functools

import jax
import jax.numpy as jnp
from jax import lax
from jax.experimental import pallas as pl
from jax.experimental.pallas import tpu as pltpu
from jax.sharding import PartitionSpec as P

HEADS = 8
HEAD_DIM = 128
W = 512
BAND = 512
CB = 256


NEG_FILL = -1e30


def passed_along(array, axis, by):
    length = lax.axis_size(axis)
    pairs = [(i, i + by) for i in range(length) if 0 <= i + by < length]
    return lax.ppermute(array, axis, pairs)


def with_halo(array, sides, width):
    for axis, dim in sides:
        size, length = (lax.axis_size(axis), array.shape[dim])
        up = [(i, (i + 1) % size) for i in range(size - 1)]
        down = [(j, i) for i, j in up]
        last = lax.slice_in_dim(array, length - width, length, axis=dim)
        first = lax.slice_in_dim(array, 0, width, axis=dim)
        before = lax.ppermute(last, axis, up)
        after = lax.ppermute(first, axis, down)
        array = jnp.concatenate([before, array, after], axis=dim)
    return array


def sent_to(array, group_flip, ctx_step):
    groups, length = (lax.axis_size("groups"), lax.axis_size("ctx"))
    pairs = [
        (g * length + c, (g ^ group_flip) * length + c + ctx_step)
        for g in range(groups)
        for c in range(length)
        if 0 <= c + ctx_step < length
    ]
    return lax.ppermute(array, ("groups", "ctx"), pairs)


def head_split(matrix):
    return matrix.reshape(matrix.shape[0], HEADS, HEAD_DIM)


def attend(queries, key_rows, value_rows, allowed, time_bias):
    scores = jnp.einsum(
        "qhd,khd->hqk",
        head_split(queries),
        head_split(key_rows),
        preferred_element_type=jnp.float32,
    ) * HEAD_DIM ** (-0.5)
    scores = jnp.where(allowed[None], scores + time_bias, NEG_FILL)
    largest = jnp.max(scores, axis=2, keepdims=True)
    exponent = jnp.exp(scores - largest)
    weights = (exponent / jnp.sum(exponent, axis=2, keepdims=True)).astype(jnp.bfloat16)
    blended = jnp.einsum(
        "hqk,khd->qhd", weights, head_split(value_rows), preferred_element_type=jnp.float32
    )
    return blended.reshape(queries.shape[0], -1)


def normalize(sem_stream, norm_gain):
    scaled = sem_stream * lax.rsqrt(
        jnp.mean(sem_stream * sem_stream, axis=1, keepdims=True) + 1e-05
    )
    return (scaled * norm_gain[None, :]).astype(jnp.bfloat16)


def contract_rows(left_side, weight_piece):
    return jnp.dot(left_side, weight_piece, preferred_element_type=jnp.float32)


def coarse_kernel(prm, slopes_ref, q_ref, k_ref, v_ref, o_ref, *, blocks, near_rows, span):
    n = pl.program_id(0)
    band_low = prm[2 * n]
    band_high = prm[2 * n + 1]
    stream_start = prm[2 * blocks]
    live_count = prm[2 * blocks + 1]
    base_row = prm[2 * blocks + 2]
    first_key = jnp.minimum(band_low - base_row, near_rows - BAND)
    step = span - BAND
    window = pl.multiple_of(jnp.clip(first_key // step * step, 0, near_rows - span), step)
    rows = n * CB + lax.broadcasted_iota(jnp.int32, (1, CB), 1)
    timing = ((stream_start + rows) // 2).astype(jnp.float32) * (2.0 / 3.0)
    key_global = base_row + window + lax.broadcasted_iota(jnp.int32, (span, 1), 0)
    inside = (key_global >= band_low) & (key_global < band_high)
    distance = jnp.where(inside, jnp.abs(timing - key_global.astype(jnp.float32)), -NEG_FILL)
    live_rows = n * CB + lax.broadcasted_iota(jnp.int32, (CB, 1), 0) < live_count
    for h in range(HEADS):
        cols = slice(h * HEAD_DIM, (h + 1) * HEAD_DIM)
        scores = lax.dot_general(
            k_ref[pl.ds(window, span), cols], q_ref[:, cols], (((1,), (1,)), ((), ())),
            preferred_element_type=jnp.float32,
        ) * HEAD_DIM ** (-0.5)
        scores = scores + distance * (-slopes_ref[h] / BAND)
        largest = jnp.max(scores, axis=0, keepdims=True)
        exponent = jnp.exp(scores - largest)
        total = jnp.sum(exponent, axis=0, keepdims=True)
        weights = (exponent * (1.0 / total)).astype(jnp.bfloat16)
        blended = lax.dot_general(
            weights, v_ref[pl.ds(window, span), cols], (((0,), (0,)), ((), ())),
            preferred_element_type=jnp.float32,
        )
        o_ref[:, cols] = jnp.where(live_rows, blended, 0.0).astype(jnp.bfloat16)


def coarse_attention(coarse_queries, near_pair, params, slopes):
    slots, width = coarse_queries.shape
    blocks = slots // CB
    near_rows = near_pair.shape[1]
    kernel = functools.partial(coarse_kernel, blocks=blocks, near_rows=near_rows, span=BAND + 128)
    grid_spec = pltpu.PrefetchScalarGridSpec(
        num_scalar_prefetch=1,
        grid=(blocks,),
        in_specs=[
            pl.BlockSpec(memory_space=pltpu.SMEM),
            pl.BlockSpec((CB, width), lambda n, prm: (n, 0)),
            pl.BlockSpec((None, near_rows, width), lambda n, prm: (prm[2 * blocks + 3], 0, 0)),
            pl.BlockSpec((None, near_rows, width), lambda n, prm: (1 - prm[2 * blocks + 3], 0, 0)),
        ],
        out_specs=pl.BlockSpec((CB, width), lambda n, prm: (n, 0)),
    )
    return pl.pallas_call(
        kernel,
        grid_spec=grid_spec,
        out_shape=jax.ShapeDtypeStruct((slots, width), jnp.bfloat16),
        compiler_params=pltpu.CompilerParams(dimension_semantics=("arbitrary",)),
    )(params, slopes, coarse_queries, near_pair, near_pair)


def on_device(
    sem_queries,
    sem_keys,
    sem_values,
    sem_inputs,
    out_proj,
    norm_gain,
    key_proj,
    value_proj,
    slopes,
    coarse_queries,
    counts,
    band_bounds,
):
    rows_here = sem_queries.shape[0]
    device_index = lax.axis_index("ctx")
    ctx_size = lax.axis_size("ctx")
    full_out_proj = lax.all_gather(out_proj, "ctx", axis=0, tiled=True)
    running = counts
    reach = 1
    while reach < ctx_size:
        running = running + passed_along(running, "ctx", reach)
        reach *= 2
    group_size = lax.axis_size("groups")
    shared = group_size % 2 == 0
    if shared:
        partners = [(i, i ^ 1) for i in range(group_size)]
        key_side = lax.axis_index("groups") % 2 == 0
        own_proj = jnp.where(key_side, key_proj, value_proj)
        gathered_proj = lax.all_gather(own_proj, "ctx", axis=0, tiled=True)
    else:
        stacked_proj = jnp.stack([key_proj, value_proj])
        gathered_proj = lax.all_gather(stacked_proj, "ctx", axis=1, tiled=True)
    own_pair = jnp.stack([sem_keys, sem_values])
    reach_shards = (W - 1 + rows_here - 1) // rows_here
    earlier = []
    for distance in range(1, reach_shards + 1):
        earlier.insert(0, passed_along(own_pair, "ctx", distance))
    window_pair = jnp.concatenate(earlier + [own_pair], axis=1)
    query_pos = jnp.arange(rows_here, dtype=jnp.int32)
    key_pos = jnp.arange(window_pair.shape[1], dtype=jnp.int32)
    key_lag = query_pos[:, None] + reach_shards * rows_here - key_pos[None, :]
    key_global = device_index * rows_here - reach_shards * rows_here + key_pos
    allowed = (key_lag >= 0) & (key_lag < W) & (key_global[None, :] >= 0)
    sem_att = attend(sem_queries, window_pair[0], window_pair[1], allowed, 0.0).astype(jnp.bfloat16)
    running, sem_att = lax.optimization_barrier((running, sem_att))
    projected = contract_rows(sem_att, full_out_proj)
    sem_stream = sem_inputs.astype(jnp.float32) + projected
    normed = normalize(sem_stream, norm_gain)
    if shared:
        partner_normed = lax.ppermute(normed, "groups", partners)
        partner_part = contract_rows(partner_normed, gathered_proj).astype(jnp.bfloat16)
        other_pieces = [sent_to(partner_part, 1, 1), sent_to(partner_part, 1, 0), sent_to(partner_part, 1, -1)]
        own_sum = contract_rows(normed, gathered_proj).astype(jnp.bfloat16)
        mine_pieces = [sent_to(own_sum, 0, 1), own_sum, sent_to(own_sum, 0, -1)]
        near_pair = jnp.concatenate(mine_pieces + other_pieces, axis=0).reshape(
            2, 3 * rows_here, own_sum.shape[1])
        key_slot = jnp.where(key_side, 0, 1)
    else:
        cross_keys = contract_rows(normed, gathered_proj[0]).astype(jnp.bfloat16)
        cross_values = contract_rows(normed, gathered_proj[1]).astype(jnp.bfloat16)
        near_pair = with_halo(jnp.stack([cross_keys, cross_values]), (("ctx", 1),), rows_here)
        key_slot = jnp.zeros((), jnp.int32)
    stream_start = (running - counts)[0]
    base_row = (device_index - 1) * rows_here
    params = jnp.concatenate(
        [band_bounds.reshape(-1).astype(jnp.int32),
         jnp.stack([stream_start, counts[0], base_row, key_slot]).astype(jnp.int32)]
    )
    return coarse_attention(coarse_queries, near_pair, params, slopes)


def solution(mesh):
    return jax.shard_map(
        on_device,
        mesh=mesh,
        in_specs=(
            P(("groups", "ctx"), None),
            P(("groups", "ctx"), None),
            P(("groups", "ctx"), None),
            P(("groups", "ctx"), None),
            P("ctx", None),
            P(),
            P("ctx", None),
            P("ctx", None),
            P(),
            P(("groups", "ctx"), None),
            P(("groups", "ctx")),
            P(("groups", "ctx"), None),
        ),
        out_specs=P(("groups", "ctx"), None),
        check_vma=False,
    )
```

```python
import functools

import jax
import jax.numpy as jnp
from jax import lax
from jax.experimental import pallas as pl
from jax.experimental.pallas import tpu as pltpu
from jax.sharding import PartitionSpec as P

HEADS = 8
HEAD_DIM = 128
W = 512
BAND = 512
CB = 256


NEG_FILL = -1e30


def passed_along(array, axis, by):
    length = lax.axis_size(axis)
    pairs = [(i, i + by) for i in range(length) if 0 <= i + by < length]
    return lax.ppermute(array, axis, pairs)


def with_halo(array, sides, width):
    for axis, dim in sides:
        size, length = (lax.axis_size(axis), array.shape[dim])
        up = [(i, (i + 1) % size) for i in range(size - 1)]
        down = [(j, i) for i, j in up]
        last = lax.slice_in_dim(array, length - width, length, axis=dim)
        first = lax.slice_in_dim(array, 0, width, axis=dim)
        before = lax.ppermute(last, axis, up)
        after = lax.ppermute(first, axis, down)
        array = jnp.concatenate([before, array, after], axis=dim)
    return array


def sent_to(array, group_flip, ctx_step):
    groups, length = (lax.axis_size("groups"), lax.axis_size("ctx"))
    pairs = [
        (g * length + c, (g ^ group_flip) * length + c + ctx_step)
        for g in range(groups)
        for c in range(length)
        if 0 <= c + ctx_step < length
    ]
    return lax.ppermute(array, ("groups", "ctx"), pairs)


def head_split(matrix):
    return matrix.reshape(matrix.shape[0], HEADS, HEAD_DIM)


def attend(queries, key_rows, value_rows, allowed, time_bias):
    scores = jnp.einsum(
        "qhd,khd->hqk",
        head_split(queries),
        head_split(key_rows),
        preferred_element_type=jnp.float32,
    ) * HEAD_DIM ** (-0.5)
    scores = jnp.where(allowed[None], scores + time_bias, NEG_FILL)
    largest = jnp.max(scores, axis=2, keepdims=True)
    exponent = jnp.exp(scores - largest)
    weights = (exponent / jnp.sum(exponent, axis=2, keepdims=True)).astype(jnp.bfloat16)
    blended = jnp.einsum(
        "hqk,khd->qhd", weights, head_split(value_rows), preferred_element_type=jnp.float32
    )
    return blended.reshape(queries.shape[0], -1)


def normalize(sem_stream, norm_gain):
    scaled = sem_stream * lax.rsqrt(
        jnp.mean(sem_stream * sem_stream, axis=1, keepdims=True) + 1e-05
    )
    return (scaled * norm_gain[None, :]).astype(jnp.bfloat16)


def contract_rows(left_side, weight_piece):
    return jnp.dot(left_side, weight_piece, preferred_element_type=jnp.float32)


def coarse_kernel(prm, slopes_ref, q_ref, k_ref, v_ref, o_ref, *, blocks, near_rows, span):
    n = pl.program_id(0)
    band_low = prm[2 * n]
    band_high = prm[2 * n + 1]
    stream_start = prm[2 * blocks]
    live_count = prm[2 * blocks + 1]
    base_row = prm[2 * blocks + 2]
    first_key = jnp.minimum(band_low - base_row, near_rows - BAND)
    step = span - BAND
    window = pl.multiple_of(jnp.clip(first_key // step * step, 0, near_rows - span), step)
    rows = n * CB + lax.broadcasted_iota(jnp.int32, (1, CB), 1)
    timing = ((stream_start + rows) // 2).astype(jnp.float32) * (2.0 / 3.0)
    key_global = base_row + window + lax.broadcasted_iota(jnp.int32, (span, 1), 0)
    inside = (key_global >= band_low) & (key_global < band_high)
    distance = jnp.where(inside, jnp.abs(timing - key_global.astype(jnp.float32)), -NEG_FILL)
    live_rows = n * CB + lax.broadcasted_iota(jnp.int32, (CB, 1), 0) < live_count
    for h in range(HEADS):
        cols = slice(h * HEAD_DIM, (h + 1) * HEAD_DIM)
        scores = lax.dot_general(
            k_ref[pl.ds(window, span), cols], q_ref[:, cols], (((1,), (1,)), ((), ())),
            preferred_element_type=jnp.float32,
        ) * HEAD_DIM ** (-0.5)
        scores = scores + distance * (-slopes_ref[h] / BAND)
        largest = jnp.max(scores, axis=0, keepdims=True)
        exponent = jnp.exp(scores - largest)
        total = jnp.sum(exponent, axis=0, keepdims=True)
        weights = (exponent * (1.0 / total)).astype(jnp.bfloat16)
        blended = lax.dot_general(
            weights, v_ref[pl.ds(window, span), cols], (((0,), (0,)), ((), ())),
            preferred_element_type=jnp.float32,
        )
        o_ref[:, cols] = jnp.where(live_rows, blended, 0.0).astype(jnp.bfloat16)


def coarse_attention(coarse_queries, near_pair, params, slopes):
    slots, width = coarse_queries.shape
    blocks = slots // CB
    near_rows = near_pair.shape[1]
    kernel = functools.partial(coarse_kernel, blocks=blocks, near_rows=near_rows, span=BAND + 128)
    grid_spec = pltpu.PrefetchScalarGridSpec(
        num_scalar_prefetch=1,
        grid=(blocks,),
        in_specs=[
            pl.BlockSpec(memory_space=pltpu.SMEM),
            pl.BlockSpec((CB, width), lambda n, prm: (n, 0)),
            pl.BlockSpec((None, near_rows, width), lambda n, prm: (prm[2 * blocks + 3], 0, 0)),
            pl.BlockSpec((None, near_rows, width), lambda n, prm: (1 - prm[2 * blocks + 3], 0, 0)),
        ],
        out_specs=pl.BlockSpec((CB, width), lambda n, prm: (n, 0)),
    )
    return pl.pallas_call(
        kernel,
        grid_spec=grid_spec,
        out_shape=jax.ShapeDtypeStruct((slots, width), jnp.bfloat16),
        compiler_params=pltpu.CompilerParams(dimension_semantics=("arbitrary",)),
    )(params, slopes, coarse_queries, near_pair, near_pair)


def on_device(
    sem_queries,
    sem_keys,
    sem_values,
    sem_inputs,
    out_proj,
    norm_gain,
    key_proj,
    value_proj,
    slopes,
    coarse_queries,
    counts,
    band_bounds,
):
    rows_here = sem_queries.shape[0]
    device_index = lax.axis_index("ctx")
    ctx_size = lax.axis_size("ctx")
    full_out_proj = lax.all_gather(out_proj, "ctx", axis=0, tiled=True)
    running = counts
    reach = 1
    while reach < ctx_size:
        running = running + passed_along(running, "ctx", reach)
        reach *= 2
    group_size = lax.axis_size("groups")
    shared = group_size % 2 == 0
    if shared:
        partners = [(i, i ^ 1) for i in range(group_size)]
        key_side = lax.axis_index("groups") % 2 == 0
        own_proj = jnp.where(key_side, key_proj, value_proj)
        gathered_proj = lax.all_gather(own_proj, "ctx", axis=0, tiled=True)
    else:
        stacked_proj = jnp.stack([key_proj, value_proj])
        gathered_proj = lax.all_gather(stacked_proj, "ctx", axis=1, tiled=True)
    own_pair = jnp.stack([sem_keys, sem_values])
    reach_shards = (W - 1 + rows_here - 1) // rows_here
    earlier = []
    for distance in range(1, reach_shards + 1):
        earlier.insert(0, passed_along(own_pair, "ctx", distance))
    window_pair = jnp.concatenate(earlier + [own_pair], axis=1)
    query_pos = jnp.arange(rows_here, dtype=jnp.int32)
    key_pos = jnp.arange(window_pair.shape[1], dtype=jnp.int32)
    key_lag = query_pos[:, None] + reach_shards * rows_here - key_pos[None, :]
    key_global = device_index * rows_here - reach_shards * rows_here + key_pos
    allowed = (key_lag >= 0) & (key_lag < W) & (key_global[None, :] >= 0)
    sem_att = attend(sem_queries, window_pair[0], window_pair[1], allowed, 0.0).astype(jnp.bfloat16)
    running, sem_att = lax.optimization_barrier((running, sem_att))
    projected = contract_rows(sem_att, full_out_proj)
    sem_stream = sem_inputs.astype(jnp.float32) + projected
    normed = normalize(sem_stream, norm_gain)
    if shared:
        partner_normed = lax.ppermute(normed, "groups", partners)
        partner_part = contract_rows(partner_normed, gathered_proj).astype(jnp.bfloat16)
        partner_sum = sent_to(partner_part, 1, 0)
        other_pieces = [sent_to(partner_sum, 0, 1), partner_sum, sent_to(partner_sum, 0, -1)]
        own_sum = contract_rows(normed, gathered_proj).astype(jnp.bfloat16)
        mine_pieces = [sent_to(own_sum, 0, 1), own_sum, sent_to(own_sum, 0, -1)]
        near_pair = jnp.concatenate(mine_pieces + other_pieces, axis=0).reshape(
            2, 3 * rows_here, own_sum.shape[1])
        key_slot = jnp.where(key_side, 0, 1)
    else:
        cross_keys = contract_rows(normed, gathered_proj[0]).astype(jnp.bfloat16)
        cross_values = contract_rows(normed, gathered_proj[1]).astype(jnp.bfloat16)
        near_pair = with_halo(jnp.stack([cross_keys, cross_values]), (("ctx", 1),), rows_here)
        key_slot = jnp.zeros((), jnp.int32)
    stream_start = (running - counts)[0]
    base_row = (device_index - 1) * rows_here
    params = jnp.concatenate(
        [band_bounds.reshape(-1).astype(jnp.int32),
         jnp.stack([stream_start, counts[0], base_row, key_slot]).astype(jnp.int32)]
    )
    return coarse_attention(coarse_queries, near_pair, params, slopes)


def solution(mesh):
    return jax.shard_map(
        on_device,
        mesh=mesh,
        in_specs=(
            P(("groups", "ctx"), None),
            P(("groups", "ctx"), None),
            P(("groups", "ctx"), None),
            P(("groups", "ctx"), None),
            P("ctx", None),
            P(),
            P("ctx", None),
            P("ctx", None),
            P(),
            P(("groups", "ctx"), None),
            P(("groups", "ctx")),
            P(("groups", "ctx"), None),
        ),
        out_specs=P(("groups", "ctx"), None),
        check_vma=False,
    )
```

```python
import functools

import jax
import jax.numpy as jnp
from jax import lax
from jax.experimental import pallas as pl
from jax.experimental.pallas import tpu as pltpu
from jax.sharding import PartitionSpec as P

HEADS = 8
HEAD_DIM = 128
W = 512
BAND = 512
CB = 256


NEG_FILL = -1e30


def passed_along(array, axis, by):
    length = lax.axis_size(axis)
    pairs = [(i, i + by) for i in range(length) if 0 <= i + by < length]
    return lax.ppermute(array, axis, pairs)


def with_halo(array, sides, width):
    for axis, dim in sides:
        size, length = (lax.axis_size(axis), array.shape[dim])
        up = [(i, (i + 1) % size) for i in range(size - 1)]
        down = [(j, i) for i, j in up]
        last = lax.slice_in_dim(array, length - width, length, axis=dim)
        first = lax.slice_in_dim(array, 0, width, axis=dim)
        before = lax.ppermute(last, axis, up)
        after = lax.ppermute(first, axis, down)
        array = jnp.concatenate([before, array, after], axis=dim)
    return array


def sent_to(array, group_flip, ctx_step):
    groups, length = (lax.axis_size("groups"), lax.axis_size("ctx"))
    pairs = [
        (g * length + c, (g ^ group_flip) * length + c + ctx_step)
        for g in range(groups)
        for c in range(length)
        if 0 <= c + ctx_step < length
    ]
    return lax.ppermute(array, ("groups", "ctx"), pairs)


def head_split(matrix):
    return matrix.reshape(matrix.shape[0], HEADS, HEAD_DIM)


def attend(queries, key_rows, value_rows, allowed, time_bias):
    scores = jnp.einsum(
        "qhd,khd->hqk",
        head_split(queries),
        head_split(key_rows),
        preferred_element_type=jnp.float32,
    ) * HEAD_DIM ** (-0.5)
    scores = jnp.where(allowed[None], scores + time_bias, NEG_FILL)
    largest = jnp.max(scores, axis=2, keepdims=True)
    exponent = jnp.exp(scores - largest)
    weights = (exponent / jnp.sum(exponent, axis=2, keepdims=True)).astype(jnp.bfloat16)
    blended = jnp.einsum(
        "hqk,khd->qhd", weights, head_split(value_rows), preferred_element_type=jnp.float32
    )
    return blended.reshape(queries.shape[0], -1)


def normalize(sem_stream, norm_gain):
    scaled = sem_stream * lax.rsqrt(
        jnp.mean(sem_stream * sem_stream, axis=1, keepdims=True) + 1e-05
    )
    return (scaled * norm_gain[None, :]).astype(jnp.bfloat16)


def contract_rows(left_side, weight_piece):
    return jnp.dot(left_side, weight_piece, preferred_element_type=jnp.float32)


def coarse_kernel(prm, slopes_ref, q_ref, k_ref, v_ref, o_ref, *, blocks, near_rows, span):
    n = pl.program_id(0)
    band_low = prm[2 * n]
    band_high = prm[2 * n + 1]
    stream_start = prm[2 * blocks]
    live_count = prm[2 * blocks + 1]
    base_row = prm[2 * blocks + 2]
    first_key = jnp.minimum(band_low - base_row, near_rows - BAND)
    step = span - BAND
    window = pl.multiple_of(jnp.clip(first_key // step * step, 0, near_rows - span), step)
    rows = n * CB + lax.broadcasted_iota(jnp.int32, (1, CB), 1)
    timing = ((stream_start + rows) // 2).astype(jnp.float32) * (2.0 / 3.0)
    key_global = base_row + window + lax.broadcasted_iota(jnp.int32, (span, 1), 0)
    inside = (key_global >= band_low) & (key_global < band_high)
    distance = jnp.where(inside, jnp.abs(timing - key_global.astype(jnp.float32)), -NEG_FILL)
    live_rows = n * CB + lax.broadcasted_iota(jnp.int32, (CB, 1), 0) < live_count
    for h in range(HEADS):
        cols = slice(h * HEAD_DIM, (h + 1) * HEAD_DIM)
        scores = lax.dot_general(
            k_ref[pl.ds(window, span), cols], q_ref[:, cols], (((1,), (1,)), ((), ())),
            preferred_element_type=jnp.float32,
        ) * HEAD_DIM ** (-0.5)
        scores = scores + distance * (-slopes_ref[h] / BAND)
        largest = jnp.max(scores, axis=0, keepdims=True)
        exponent = jnp.exp(scores - largest)
        total = jnp.sum(exponent, axis=0, keepdims=True)
        weights = (exponent * (1.0 / total)).astype(jnp.bfloat16)
        blended = lax.dot_general(
            weights, v_ref[pl.ds(window, span), cols], (((0,), (0,)), ((), ())),
            preferred_element_type=jnp.float32,
        )
        o_ref[:, cols] = jnp.where(live_rows, blended, 0.0).astype(jnp.bfloat16)


def coarse_attention(coarse_queries, near_pair, params, slopes):
    slots, width = coarse_queries.shape
    blocks = slots // CB
    near_rows = near_pair.shape[1]
    kernel = functools.partial(coarse_kernel, blocks=blocks, near_rows=near_rows, span=BAND + 128)
    grid_spec = pltpu.PrefetchScalarGridSpec(
        num_scalar_prefetch=1,
        grid=(blocks,),
        in_specs=[
            pl.BlockSpec(memory_space=pltpu.SMEM),
            pl.BlockSpec((CB, width), lambda n, prm: (n, 0)),
            pl.BlockSpec((None, near_rows, width), lambda n, prm: (prm[2 * blocks + 3], 0, 0)),
            pl.BlockSpec((None, near_rows, width), lambda n, prm: (1 - prm[2 * blocks + 3], 0, 0)),
        ],
        out_specs=pl.BlockSpec((CB, width), lambda n, prm: (n, 0)),
    )
    return pl.pallas_call(
        kernel,
        grid_spec=grid_spec,
        out_shape=jax.ShapeDtypeStruct((slots, width), jnp.bfloat16),
        compiler_params=pltpu.CompilerParams(dimension_semantics=("arbitrary",)),
    )(params, slopes, coarse_queries, near_pair, near_pair)


def on_device(
    sem_queries,
    sem_keys,
    sem_values,
    sem_inputs,
    out_proj,
    norm_gain,
    key_proj,
    value_proj,
    slopes,
    coarse_queries,
    counts,
    band_bounds,
):
    rows_here = sem_queries.shape[0]
    device_index = lax.axis_index("ctx")
    ctx_size = lax.axis_size("ctx")
    full_out_proj = lax.all_gather(out_proj, "ctx", axis=0, tiled=True)
    running = counts
    reach = 1
    while reach < ctx_size:
        running = running + passed_along(running, "ctx", reach)
        reach *= 2
    group_size = lax.axis_size("groups")
    shared = group_size % 2 == 0
    if shared:
        partners = [(i, i ^ 1) for i in range(group_size)]
        key_side = lax.axis_index("groups") % 2 == 0
        own_proj = jnp.where(key_side, key_proj, value_proj)
        gathered_proj = lax.all_gather(own_proj, "ctx", axis=0, tiled=True)
    else:
        stacked_proj = jnp.stack([key_proj, value_proj])
        gathered_proj = lax.all_gather(stacked_proj, "ctx", axis=1, tiled=True)
    own_pair = jnp.stack([sem_keys, sem_values])
    full_out_proj, own_pair = lax.optimization_barrier((full_out_proj, own_pair))
    reach_shards = (W - 1 + rows_here - 1) // rows_here
    earlier = []
    for distance in range(1, reach_shards + 1):
        earlier.insert(0, passed_along(own_pair, "ctx", distance))
    window_pair = jnp.concatenate(earlier + [own_pair], axis=1)
    query_pos = jnp.arange(rows_here, dtype=jnp.int32)
    key_pos = jnp.arange(window_pair.shape[1], dtype=jnp.int32)
    key_lag = query_pos[:, None] + reach_shards * rows_here - key_pos[None, :]
    key_global = device_index * rows_here - reach_shards * rows_here + key_pos
    allowed = (key_lag >= 0) & (key_lag < W) & (key_global[None, :] >= 0)
    sem_att = attend(sem_queries, window_pair[0], window_pair[1], allowed, 0.0).astype(jnp.bfloat16)
    running, sem_att = lax.optimization_barrier((running, sem_att))
    projected = contract_rows(sem_att, full_out_proj)
    sem_stream = sem_inputs.astype(jnp.float32) + projected
    normed = normalize(sem_stream, norm_gain)
    if shared:
        partner_normed = lax.ppermute(normed, "groups", partners)
        partner_part = contract_rows(partner_normed, gathered_proj).astype(jnp.bfloat16)
        partner_sum = sent_to(partner_part, 1, 0)
        other_pieces = [sent_to(partner_sum, 0, 1), partner_sum, sent_to(partner_sum, 0, -1)]
        own_sum = contract_rows(normed, gathered_proj).astype(jnp.bfloat16)
        mine_pieces = [sent_to(own_sum, 0, 1), own_sum, sent_to(own_sum, 0, -1)]
        near_pair = jnp.concatenate(mine_pieces + other_pieces, axis=0).reshape(
            2, 3 * rows_here, own_sum.shape[1])
        key_slot = jnp.where(key_side, 0, 1)
    else:
        cross_keys = contract_rows(normed, gathered_proj[0]).astype(jnp.bfloat16)
        cross_values = contract_rows(normed, gathered_proj[1]).astype(jnp.bfloat16)
        near_pair = with_halo(jnp.stack([cross_keys, cross_values]), (("ctx", 1),), rows_here)
        key_slot = jnp.zeros((), jnp.int32)
    stream_start = (running - counts)[0]
    base_row = (device_index - 1) * rows_here
    params = jnp.concatenate(
        [band_bounds.reshape(-1).astype(jnp.int32),
         jnp.stack([stream_start, counts[0], base_row, key_slot]).astype(jnp.int32)]
    )
    return coarse_attention(coarse_queries, near_pair, params, slopes)


def solution(mesh):
    return jax.shard_map(
        on_device,
        mesh=mesh,
        in_specs=(
            P(("groups", "ctx"), None),
            P(("groups", "ctx"), None),
            P(("groups", "ctx"), None),
            P(("groups", "ctx"), None),
            P("ctx", None),
            P(),
            P("ctx", None),
            P("ctx", None),
            P(),
            P(("groups", "ctx"), None),
            P(("groups", "ctx")),
            P(("groups", "ctx"), None),
        ),
        out_specs=P(("groups", "ctx"), None),
        check_vma=False,
    )
```

```python
import functools

import jax
import jax.numpy as jnp
from jax import lax
from jax.experimental import pallas as pl
from jax.experimental.pallas import tpu as pltpu
from jax.sharding import PartitionSpec as P

HEADS = 8
HEAD_DIM = 128
W = 512
BAND = 512
CB = 256


NEG_FILL = -1e30


def passed_along(array, axis, by):
    length = lax.axis_size(axis)
    pairs = [(i, i + by) for i in range(length) if 0 <= i + by < length]
    return lax.ppermute(array, axis, pairs)


def with_halo(array, sides, width):
    for axis, dim in sides:
        size, length = (lax.axis_size(axis), array.shape[dim])
        up = [(i, (i + 1) % size) for i in range(size - 1)]
        down = [(j, i) for i, j in up]
        last = lax.slice_in_dim(array, length - width, length, axis=dim)
        first = lax.slice_in_dim(array, 0, width, axis=dim)
        before = lax.ppermute(last, axis, up)
        after = lax.ppermute(first, axis, down)
        array = jnp.concatenate([before, array, after], axis=dim)
    return array


def sent_to(array, group_flip, ctx_step):
    groups, length = (lax.axis_size("groups"), lax.axis_size("ctx"))
    pairs = [
        (g * length + c, (g ^ group_flip) * length + c + ctx_step)
        for g in range(groups)
        for c in range(length)
        if 0 <= c + ctx_step < length
    ]
    return lax.ppermute(array, ("groups", "ctx"), pairs)


def head_split(matrix):
    return matrix.reshape(matrix.shape[0], HEADS, HEAD_DIM)


def attend(queries, key_rows, value_rows, allowed, time_bias):
    scores = jnp.einsum(
        "qhd,khd->hqk",
        head_split(queries),
        head_split(key_rows),
        preferred_element_type=jnp.float32,
    ) * HEAD_DIM ** (-0.5)
    scores = jnp.where(allowed[None], scores + time_bias, NEG_FILL)
    largest = jnp.max(scores, axis=2, keepdims=True)
    exponent = jnp.exp(scores - largest)
    weights = (exponent / jnp.sum(exponent, axis=2, keepdims=True)).astype(jnp.bfloat16)
    blended = jnp.einsum(
        "hqk,khd->qhd", weights, head_split(value_rows), preferred_element_type=jnp.float32
    )
    return blended.reshape(queries.shape[0], -1)


def normalize(sem_stream, norm_gain):
    scaled = sem_stream * lax.rsqrt(
        jnp.mean(sem_stream * sem_stream, axis=1, keepdims=True) + 1e-05
    )
    return (scaled * norm_gain[None, :]).astype(jnp.bfloat16)


def contract_rows(left_side, weight_piece):
    return jnp.dot(left_side, weight_piece, preferred_element_type=jnp.float32)


def coarse_kernel(prm, slopes_ref, q_ref, k_ref, v_ref, o_ref, *, blocks, near_rows, span):
    n = pl.program_id(0)
    band_low = prm[2 * n]
    band_high = prm[2 * n + 1]
    stream_start = prm[2 * blocks]
    live_count = prm[2 * blocks + 1]
    base_row = prm[2 * blocks + 2]
    first_key = jnp.minimum(band_low - base_row, near_rows - BAND)
    step = span - BAND
    window = pl.multiple_of(jnp.clip(first_key // step * step, 0, near_rows - span), step)
    rows = n * CB + lax.broadcasted_iota(jnp.int32, (1, CB), 1)
    timing = ((stream_start + rows) // 2).astype(jnp.float32) * (2.0 / 3.0)
    key_global = base_row + window + lax.broadcasted_iota(jnp.int32, (span, 1), 0)
    inside = (key_global >= band_low) & (key_global < band_high)
    distance = jnp.where(inside, jnp.abs(timing - key_global.astype(jnp.float32)), -NEG_FILL)
    live_rows = n * CB + lax.broadcasted_iota(jnp.int32, (CB, 1), 0) < live_count
    for h in range(HEADS):
        cols = slice(h * HEAD_DIM, (h + 1) * HEAD_DIM)
        scores = lax.dot_general(
            k_ref[pl.ds(window, span), cols], q_ref[:, cols], (((1,), (1,)), ((), ())),
            preferred_element_type=jnp.float32,
        ) * HEAD_DIM ** (-0.5)
        scores = scores + distance * (-slopes_ref[h] / BAND)
        largest = jnp.max(scores, axis=0, keepdims=True)
        exponent = jnp.exp(scores - largest)
        total = jnp.sum(exponent, axis=0, keepdims=True)
        weights = (exponent * (1.0 / total)).astype(jnp.bfloat16)
        blended = lax.dot_general(
            weights, v_ref[pl.ds(window, span), cols], (((0,), (0,)), ((), ())),
            preferred_element_type=jnp.float32,
        )
        o_ref[:, cols] = jnp.where(live_rows, blended, 0.0).astype(jnp.bfloat16)


def coarse_attention(coarse_queries, near_pair, params, slopes):
    slots, width = coarse_queries.shape
    blocks = slots // CB
    near_rows = near_pair.shape[1]
    kernel = functools.partial(coarse_kernel, blocks=blocks, near_rows=near_rows, span=BAND + 128)
    grid_spec = pltpu.PrefetchScalarGridSpec(
        num_scalar_prefetch=1,
        grid=(blocks,),
        in_specs=[
            pl.BlockSpec(memory_space=pltpu.SMEM),
            pl.BlockSpec((CB, width), lambda n, prm: (n, 0)),
            pl.BlockSpec((None, near_rows, width), lambda n, prm: (prm[2 * blocks + 3], 0, 0)),
            pl.BlockSpec((None, near_rows, width), lambda n, prm: (1 - prm[2 * blocks + 3], 0, 0)),
        ],
        out_specs=pl.BlockSpec((CB, width), lambda n, prm: (n, 0)),
    )
    return pl.pallas_call(
        kernel,
        grid_spec=grid_spec,
        out_shape=jax.ShapeDtypeStruct((slots, width), jnp.bfloat16),
        compiler_params=pltpu.CompilerParams(dimension_semantics=("arbitrary",)),
    )(params, slopes, coarse_queries, near_pair, near_pair)


def on_device(
    sem_queries,
    sem_keys,
    sem_values,
    sem_inputs,
    out_proj,
    norm_gain,
    key_proj,
    value_proj,
    slopes,
    coarse_queries,
    counts,
    band_bounds,
):
    rows_here = sem_queries.shape[0]
    device_index = lax.axis_index("ctx")
    ctx_size = lax.axis_size("ctx")
    full_out_proj = lax.all_gather(out_proj, "ctx", axis=0, tiled=True)
    running = counts
    reach = 1
    while reach < ctx_size:
        running = running + passed_along(running, "ctx", reach)
        reach *= 2
    group_size = lax.axis_size("groups")
    shared = group_size % 2 == 0
    if shared:
        partners = [(i, i ^ 1) for i in range(group_size)]
        key_side = lax.axis_index("groups") % 2 == 0
        own_proj = jnp.where(key_side, key_proj, value_proj)
        gathered_proj = lax.all_gather(own_proj, "ctx", axis=0, tiled=True)
    else:
        stacked_proj = jnp.stack([key_proj, value_proj])
        gathered_proj = lax.all_gather(stacked_proj, "ctx", axis=1, tiled=True)
    own_pair = jnp.stack([sem_keys, sem_values])
    reach_shards = (W - 1 + rows_here - 1) // rows_here
    earlier = []
    for distance in range(1, reach_shards + 1):
        earlier.insert(0, passed_along(own_pair, "ctx", distance))
    window_pair = jnp.concatenate(earlier + [own_pair], axis=1)
    query_pos = jnp.arange(rows_here, dtype=jnp.int32)
    key_pos = jnp.arange(window_pair.shape[1], dtype=jnp.int32)
    key_lag = query_pos[:, None] + reach_shards * rows_here - key_pos[None, :]
    key_global = device_index * rows_here - reach_shards * rows_here + key_pos
    allowed = (key_lag >= 0) & (key_lag < W) & (key_global[None, :] >= 0)
    sem_att = attend(sem_queries, window_pair[0], window_pair[1], allowed, 0.0).astype(jnp.bfloat16)
    running, sem_att = lax.optimization_barrier((running, sem_att))
    projected = contract_rows(sem_att, full_out_proj)
    sem_stream = sem_inputs.astype(jnp.float32) + projected
    normed = normalize(sem_stream, norm_gain)
    if shared:
        partner_normed = lax.ppermute(normed, "groups", partners)
        partner_part = contract_rows(partner_normed, gathered_proj).astype(jnp.bfloat16)
        partner_sum = sent_to(partner_part, 1, 0)
        other_pieces = [sent_to(partner_sum, 0, 1), partner_sum, sent_to(partner_sum, 0, -1)]
        partner_part, normed = lax.optimization_barrier((partner_part, normed))
        own_sum = contract_rows(normed, gathered_proj).astype(jnp.bfloat16)
        mine_pieces = [sent_to(own_sum, 0, 1), own_sum, sent_to(own_sum, 0, -1)]
        near_pair = jnp.concatenate(mine_pieces + other_pieces, axis=0).reshape(
            2, 3 * rows_here, own_sum.shape[1])
        key_slot = jnp.where(key_side, 0, 1)
    else:
        cross_keys = contract_rows(normed, gathered_proj[0]).astype(jnp.bfloat16)
        cross_values = contract_rows(normed, gathered_proj[1]).astype(jnp.bfloat16)
        near_pair = with_halo(jnp.stack([cross_keys, cross_values]), (("ctx", 1),), rows_here)
        key_slot = jnp.zeros((), jnp.int32)
    stream_start = (running - counts)[0]
    base_row = (device_index - 1) * rows_here
    params = jnp.concatenate(
        [band_bounds.reshape(-1).astype(jnp.int32),
         jnp.stack([stream_start, counts[0], base_row, key_slot]).astype(jnp.int32)]
    )
    return coarse_attention(coarse_queries, near_pair, params, slopes)


def solution(mesh):
    return jax.shard_map(
        on_device,
        mesh=mesh,
        in_specs=(
            P(("groups", "ctx"), None),
            P(("groups", "ctx"), None),
            P(("groups", "ctx"), None),
            P(("groups", "ctx"), None),
            P("ctx", None),
            P(),
            P("ctx", None),
            P("ctx", None),
            P(),
            P(("groups", "ctx"), None),
            P(("groups", "ctx")),
            P(("groups", "ctx"), None),
        ),
        out_specs=P(("groups", "ctx"), None),
        check_vma=False,
    )
```

```python
import functools

import jax
import jax.numpy as jnp
from jax import lax
from jax.experimental import pallas as pl
from jax.experimental.pallas import tpu as pltpu
from jax.sharding import PartitionSpec as P

HEADS = 8
HEAD_DIM = 128
W = 512
BAND = 512
CB = 256


NEG_FILL = -1e30


def passed_along(array, axis, by):
    length = lax.axis_size(axis)
    pairs = [(i, i + by) for i in range(length) if 0 <= i + by < length]
    return lax.ppermute(array, axis, pairs)


def with_halo(array, sides, width):
    for axis, dim in sides:
        size, length = (lax.axis_size(axis), array.shape[dim])
        up = [(i, (i + 1) % size) for i in range(size - 1)]
        down = [(j, i) for i, j in up]
        last = lax.slice_in_dim(array, length - width, length, axis=dim)
        first = lax.slice_in_dim(array, 0, width, axis=dim)
        before = lax.ppermute(last, axis, up)
        after = lax.ppermute(first, axis, down)
        array = jnp.concatenate([before, array, after], axis=dim)
    return array


def sent_to(array, group_flip, ctx_step):
    groups, length = (lax.axis_size("groups"), lax.axis_size("ctx"))
    pairs = [
        (g * length + c, (g ^ group_flip) * length + c + ctx_step)
        for g in range(groups)
        for c in range(length)
        if 0 <= c + ctx_step < length
    ]
    return lax.ppermute(array, ("groups", "ctx"), pairs)


def head_split(matrix):
    return matrix.reshape(matrix.shape[0], HEADS, HEAD_DIM)


def attend(queries, key_rows, value_rows, allowed, time_bias):
    scores = jnp.einsum(
        "qhd,khd->hqk",
        head_split(queries),
        head_split(key_rows),
        preferred_element_type=jnp.float32,
    ) * HEAD_DIM ** (-0.5)
    scores = jnp.where(allowed[None], scores + time_bias, NEG_FILL)
    largest = jnp.max(scores, axis=2, keepdims=True)
    exponent = jnp.exp(scores - largest)
    weights = (exponent / jnp.sum(exponent, axis=2, keepdims=True)).astype(jnp.bfloat16)
    blended = jnp.einsum(
        "hqk,khd->qhd", weights, head_split(value_rows), preferred_element_type=jnp.float32
    )
    return blended.reshape(queries.shape[0], -1)


def normalize(sem_stream, norm_gain):
    scaled = sem_stream * lax.rsqrt(
        jnp.mean(sem_stream * sem_stream, axis=1, keepdims=True) + 1e-05
    )
    return (scaled * norm_gain[None, :]).astype(jnp.bfloat16)


def contract_rows(left_side, weight_piece):
    return jnp.dot(left_side, weight_piece, preferred_element_type=jnp.float32)


def coarse_kernel(prm, slopes_ref, q_ref, k_ref, v_ref, o_ref, *, blocks, near_rows, span):
    n = pl.program_id(0)
    band_low = prm[2 * n]
    band_high = prm[2 * n + 1]
    stream_start = prm[2 * blocks]
    live_count = prm[2 * blocks + 1]
    base_row = prm[2 * blocks + 2]
    first_key = jnp.minimum(band_low - base_row, near_rows - BAND)
    step = span - BAND
    window = pl.multiple_of(jnp.clip(first_key // step * step, 0, near_rows - span), step)
    rows = n * CB + lax.broadcasted_iota(jnp.int32, (1, CB), 1)
    timing = ((stream_start + rows) // 2).astype(jnp.float32) * (2.0 / 3.0)
    key_global = base_row + window + lax.broadcasted_iota(jnp.int32, (span, 1), 0)
    inside = (key_global >= band_low) & (key_global < band_high)
    distance = jnp.where(inside, jnp.abs(timing - key_global.astype(jnp.float32)), -NEG_FILL)
    live_rows = n * CB + lax.broadcasted_iota(jnp.int32, (CB, 1), 0) < live_count
    for h in range(HEADS):
        cols = slice(h * HEAD_DIM, (h + 1) * HEAD_DIM)
        scores = lax.dot_general(
            k_ref[pl.ds(window, span), cols], q_ref[:, cols], (((1,), (1,)), ((), ())),
            preferred_element_type=jnp.float32,
        ) * HEAD_DIM ** (-0.5)
        scores = scores + distance * (-slopes_ref[h] / BAND)
        largest = jnp.max(scores, axis=0, keepdims=True)
        exponent = jnp.exp(scores - largest)
        total = jnp.sum(exponent, axis=0, keepdims=True)
        weights = (exponent * (1.0 / total)).astype(jnp.bfloat16)
        blended = lax.dot_general(
            weights, v_ref[pl.ds(window, span), cols], (((0,), (0,)), ((), ())),
            preferred_element_type=jnp.float32,
        )
        o_ref[:, cols] = jnp.where(live_rows, blended, 0.0).astype(jnp.bfloat16)


def coarse_attention(coarse_queries, near_pair, params, slopes):
    slots, width = coarse_queries.shape
    blocks = slots // CB
    near_rows = near_pair.shape[1]
    kernel = functools.partial(coarse_kernel, blocks=blocks, near_rows=near_rows, span=BAND + 128)
    grid_spec = pltpu.PrefetchScalarGridSpec(
        num_scalar_prefetch=1,
        grid=(blocks,),
        in_specs=[
            pl.BlockSpec(memory_space=pltpu.SMEM),
            pl.BlockSpec((CB, width), lambda n, prm: (n, 0)),
            pl.BlockSpec((None, near_rows, width), lambda n, prm: (prm[2 * blocks + 3], 0, 0)),
            pl.BlockSpec((None, near_rows, width), lambda n, prm: (1 - prm[2 * blocks + 3], 0, 0)),
        ],
        out_specs=pl.BlockSpec((CB, width), lambda n, prm: (n, 0)),
    )
    return pl.pallas_call(
        kernel,
        grid_spec=grid_spec,
        out_shape=jax.ShapeDtypeStruct((slots, width), jnp.bfloat16),
        compiler_params=pltpu.CompilerParams(dimension_semantics=("arbitrary",)),
    )(params, slopes, coarse_queries, near_pair, near_pair)


def on_device(
    sem_queries,
    sem_keys,
    sem_values,
    sem_inputs,
    out_proj,
    norm_gain,
    key_proj,
    value_proj,
    slopes,
    coarse_queries,
    counts,
    band_bounds,
):
    rows_here = sem_queries.shape[0]
    device_index = lax.axis_index("ctx")
    ctx_size = lax.axis_size("ctx")
    full_out_proj = lax.all_gather(out_proj, "ctx", axis=0, tiled=True)
    running = counts
    reach = 1
    while reach < ctx_size:
        running = running + passed_along(running, "ctx", reach)
        reach *= 2
    group_size = lax.axis_size("groups")
    shared = group_size % 2 == 0
    if shared:
        partners = [(i, i ^ 1) for i in range(group_size)]
        key_side = lax.axis_index("groups") % 2 == 0
        own_proj = jnp.where(key_side, key_proj, value_proj)
        gathered_proj = lax.all_gather(own_proj, "ctx", axis=0, tiled=True)
    else:
        stacked_proj = jnp.stack([key_proj, value_proj])
        gathered_proj = lax.all_gather(stacked_proj, "ctx", axis=1, tiled=True)
    own_pair = jnp.stack([sem_keys, sem_values])
    reach_shards = (W - 1 + rows_here - 1) // rows_here
    earlier = []
    relayed = own_pair
    for distance in range(1, reach_shards + 1):
        relayed = passed_along(relayed, "ctx", 1)
        earlier.insert(0, relayed)
    window_pair = jnp.concatenate(earlier + [own_pair], axis=1)
    query_pos = jnp.arange(rows_here, dtype=jnp.int32)
    key_pos = jnp.arange(window_pair.shape[1], dtype=jnp.int32)
    key_lag = query_pos[:, None] + reach_shards * rows_here - key_pos[None, :]
    key_global = device_index * rows_here - reach_shards * rows_here + key_pos
    allowed = (key_lag >= 0) & (key_lag < W) & (key_global[None, :] >= 0)
    sem_att = attend(sem_queries, window_pair[0], window_pair[1], allowed, 0.0).astype(jnp.bfloat16)
    running, sem_att = lax.optimization_barrier((running, sem_att))
    projected = contract_rows(sem_att, full_out_proj)
    sem_stream = sem_inputs.astype(jnp.float32) + projected
    normed = normalize(sem_stream, norm_gain)
    if shared:
        partner_normed = lax.ppermute(normed, "groups", partners)
        partner_part = contract_rows(partner_normed, gathered_proj).astype(jnp.bfloat16)
        partner_sum = sent_to(partner_part, 1, 0)
        other_pieces = [sent_to(partner_sum, 0, 1), partner_sum, sent_to(partner_sum, 0, -1)]
        own_sum = contract_rows(normed, gathered_proj).astype(jnp.bfloat16)
        mine_pieces = [sent_to(own_sum, 0, 1), own_sum, sent_to(own_sum, 0, -1)]
        near_pair = jnp.concatenate(mine_pieces + other_pieces, axis=0).reshape(
            2, 3 * rows_here, own_sum.shape[1])
        key_slot = jnp.where(key_side, 0, 1)
    else:
        cross_keys = contract_rows(normed, gathered_proj[0]).astype(jnp.bfloat16)
        cross_values = contract_rows(normed, gathered_proj[1]).astype(jnp.bfloat16)
        near_pair = with_halo(jnp.stack([cross_keys, cross_values]), (("ctx", 1),), rows_here)
        key_slot = jnp.zeros((), jnp.int32)
    stream_start = (running - counts)[0]
    base_row = (device_index - 1) * rows_here
    params = jnp.concatenate(
        [band_bounds.reshape(-1).astype(jnp.int32),
         jnp.stack([stream_start, counts[0], base_row, key_slot]).astype(jnp.int32)]
    )
    return coarse_attention(coarse_queries, near_pair, params, slopes)


def solution(mesh):
    return jax.shard_map(
        on_device,
        mesh=mesh,
        in_specs=(
            P(("groups", "ctx"), None),
            P(("groups", "ctx"), None),
            P(("groups", "ctx"), None),
            P(("groups", "ctx"), None),
            P("ctx", None),
            P(),
            P("ctx", None),
            P("ctx", None),
            P(),
            P(("groups", "ctx"), None),
            P(("groups", "ctx")),
            P(("groups", "ctx"), None),
        ),
        out_specs=P(("groups", "ctx"), None),
        check_vma=False,
    )
```

```python
import functools

import jax
import jax.numpy as jnp
from jax import lax
from jax.experimental import pallas as pl
from jax.experimental.pallas import tpu as pltpu
from jax.sharding import PartitionSpec as P

HEADS = 8
HEAD_DIM = 128
W = 512
BAND = 512
CB = 256


NEG_FILL = -1e30


def passed_along(array, axis, by):
    length = lax.axis_size(axis)
    pairs = [(i, i + by) for i in range(length) if 0 <= i + by < length]
    return lax.ppermute(array, axis, pairs)


def with_halo(array, sides, width):
    for axis, dim in sides:
        size, length = (lax.axis_size(axis), array.shape[dim])
        up = [(i, (i + 1) % size) for i in range(size - 1)]
        down = [(j, i) for i, j in up]
        last = lax.slice_in_dim(array, length - width, length, axis=dim)
        first = lax.slice_in_dim(array, 0, width, axis=dim)
        before = lax.ppermute(last, axis, up)
        after = lax.ppermute(first, axis, down)
        array = jnp.concatenate([before, array, after], axis=dim)
    return array


def sent_to(array, group_flip, ctx_step):
    groups, length = (lax.axis_size("groups"), lax.axis_size("ctx"))
    pairs = [
        (g * length + c, (g ^ group_flip) * length + c + ctx_step)
        for g in range(groups)
        for c in range(length)
        if 0 <= c + ctx_step < length
    ]
    return lax.ppermute(array, ("groups", "ctx"), pairs)


def head_split(matrix):
    return matrix.reshape(matrix.shape[0], HEADS, HEAD_DIM)


def attend(queries, key_rows, value_rows, allowed, time_bias):
    scores = jnp.einsum(
        "qhd,khd->hqk",
        head_split(queries),
        head_split(key_rows),
        preferred_element_type=jnp.float32,
    ) * HEAD_DIM ** (-0.5)
    scores = jnp.where(allowed[None], scores + time_bias, NEG_FILL)
    largest = jnp.max(scores, axis=2, keepdims=True)
    exponent = jnp.exp(scores - largest)
    weights = (exponent / jnp.sum(exponent, axis=2, keepdims=True)).astype(jnp.bfloat16)
    blended = jnp.einsum(
        "hqk,khd->qhd", weights, head_split(value_rows), preferred_element_type=jnp.float32
    )
    return blended.reshape(queries.shape[0], -1)


def normalize(sem_stream, norm_gain):
    scaled = sem_stream * lax.rsqrt(
        jnp.mean(sem_stream * sem_stream, axis=1, keepdims=True) + 1e-05
    )
    return (scaled * norm_gain[None, :]).astype(jnp.bfloat16)


def contract_rows(left_side, weight_piece):
    return jnp.dot(left_side, weight_piece, preferred_element_type=jnp.float32)


def coarse_kernel(prm, slopes_ref, q_ref, k_ref, v_ref, o_ref, *, blocks, near_rows, span):
    n = pl.program_id(0)
    band_low = prm[2 * n]
    band_high = prm[2 * n + 1]
    stream_start = prm[2 * blocks]
    live_count = prm[2 * blocks + 1]
    base_row = prm[2 * blocks + 2]
    first_key = jnp.minimum(band_low - base_row, near_rows - BAND)
    step = span - BAND
    window = pl.multiple_of(jnp.clip(first_key // step * step, 0, near_rows - span), step)
    rows = n * CB + lax.broadcasted_iota(jnp.int32, (1, CB), 1)
    timing = ((stream_start + rows) // 2).astype(jnp.float32) * (2.0 / 3.0)
    key_global = base_row + window + lax.broadcasted_iota(jnp.int32, (span, 1), 0)
    inside = (key_global >= band_low) & (key_global < band_high)
    distance = jnp.where(inside, jnp.abs(timing - key_global.astype(jnp.float32)), -NEG_FILL)
    live_rows = n * CB + lax.broadcasted_iota(jnp.int32, (CB, 1), 0) < live_count
    for h in range(HEADS):
        cols = slice(h * HEAD_DIM, (h + 1) * HEAD_DIM)
        scores = lax.dot_general(
            k_ref[pl.ds(window, span), cols], q_ref[:, cols], (((1,), (1,)), ((), ())),
            preferred_element_type=jnp.float32,
        ) * HEAD_DIM ** (-0.5)
        scores = scores + distance * (-slopes_ref[h] / BAND)
        largest = jnp.max(scores, axis=0, keepdims=True)
        exponent = jnp.exp(scores - largest)
        total = jnp.sum(exponent, axis=0, keepdims=True)
        weights = (exponent * (1.0 / total)).astype(jnp.bfloat16)
        blended = lax.dot_general(
            weights, v_ref[pl.ds(window, span), cols], (((0,), (0,)), ((), ())),
            preferred_element_type=jnp.float32,
        )
        o_ref[:, cols] = jnp.where(live_rows, blended, 0.0).astype(jnp.bfloat16)


def coarse_attention(coarse_queries, near_pair, params, slopes):
    slots, width = coarse_queries.shape
    blocks = slots // CB
    near_rows = near_pair.shape[1]
    kernel = functools.partial(coarse_kernel, blocks=blocks, near_rows=near_rows, span=BAND + 128)
    grid_spec = pltpu.PrefetchScalarGridSpec(
        num_scalar_prefetch=1,
        grid=(blocks,),
        in_specs=[
            pl.BlockSpec(memory_space=pltpu.SMEM),
            pl.BlockSpec((CB, width), lambda n, prm: (n, 0)),
            pl.BlockSpec((None, near_rows, width), lambda n, prm: (prm[2 * blocks + 3], 0, 0)),
            pl.BlockSpec((None, near_rows, width), lambda n, prm: (1 - prm[2 * blocks + 3], 0, 0)),
        ],
        out_specs=pl.BlockSpec((CB, width), lambda n, prm: (n, 0)),
    )
    return pl.pallas_call(
        kernel,
        grid_spec=grid_spec,
        out_shape=jax.ShapeDtypeStruct((slots, width), jnp.bfloat16),
        compiler_params=pltpu.CompilerParams(dimension_semantics=("arbitrary",)),
    )(params, slopes, coarse_queries, near_pair, near_pair)


def on_device(
    sem_queries,
    sem_keys,
    sem_values,
    sem_inputs,
    out_proj,
    norm_gain,
    key_proj,
    value_proj,
    slopes,
    coarse_queries,
    counts,
    band_bounds,
):
    rows_here = sem_queries.shape[0]
    device_index = lax.axis_index("ctx")
    ctx_size = lax.axis_size("ctx")
    full_out_proj = lax.all_gather(out_proj, "ctx", axis=0, tiled=True)
    running = counts
    reach = 1
    while reach < ctx_size:
        running = running + passed_along(running, "ctx", reach)
        reach *= 2
    group_size = lax.axis_size("groups")
    shared = group_size % 2 == 0
    if shared:
        partners = [(i, i ^ 1) for i in range(group_size)]
        key_side = lax.axis_index("groups") % 2 == 0
        own_proj = jnp.where(key_side, key_proj, value_proj)
        gathered_proj = lax.all_gather(own_proj, "ctx", axis=0, tiled=True)
    else:
        stacked_proj = jnp.stack([key_proj, value_proj])
        gathered_proj = lax.all_gather(stacked_proj, "ctx", axis=1, tiled=True)
    own_pair = jnp.stack([sem_keys, sem_values])
    reach_shards = (W - 1 + rows_here - 1) // rows_here
    earlier = []
    relayed = own_pair
    for distance in range(1, reach_shards + 1):
        relayed = passed_along(relayed, "ctx", 1)
        earlier.insert(0, relayed)
    window_pair = jnp.concatenate(earlier + [own_pair], axis=1)
    query_pos = jnp.arange(rows_here, dtype=jnp.int32)
    key_pos = jnp.arange(window_pair.shape[1], dtype=jnp.int32)
    key_lag = query_pos[:, None] + reach_shards * rows_here - key_pos[None, :]
    key_global = device_index * rows_here - reach_shards * rows_here + key_pos
    allowed = (key_lag >= 0) & (key_lag < W) & (key_global[None, :] >= 0)
    sem_att = attend(sem_queries, window_pair[0], window_pair[1], allowed, 0.0).astype(jnp.bfloat16)
    running, sem_att = lax.optimization_barrier((running, sem_att))
    projected = contract_rows(sem_att, full_out_proj)
    sem_stream = sem_inputs.astype(jnp.float32) + projected
    normed = normalize(sem_stream, norm_gain)
    if shared:
        partner_normed = lax.ppermute(normed, "groups", partners)
        partner_part = contract_rows(partner_normed, gathered_proj).astype(jnp.bfloat16)
        halves = [sent_to(part, 1, 0) for part in jnp.split(partner_part, 2, axis=0)]
        partner_sum = jnp.concatenate(halves, axis=0)
        other_pieces = [
            jnp.concatenate([sent_to(part, 0, 1) for part in halves], axis=0),
            partner_sum,
            jnp.concatenate([sent_to(part, 0, -1) for part in halves], axis=0),
        ]
        own_sum = contract_rows(normed, gathered_proj).astype(jnp.bfloat16)
        mine_pieces = [sent_to(own_sum, 0, 1), own_sum, sent_to(own_sum, 0, -1)]
        near_pair = jnp.concatenate(mine_pieces + other_pieces, axis=0).reshape(
            2, 3 * rows_here, own_sum.shape[1])
        key_slot = jnp.where(key_side, 0, 1)
    else:
        cross_keys = contract_rows(normed, gathered_proj[0]).astype(jnp.bfloat16)
        cross_values = contract_rows(normed, gathered_proj[1]).astype(jnp.bfloat16)
        near_pair = with_halo(jnp.stack([cross_keys, cross_values]), (("ctx", 1),), rows_here)
        key_slot = jnp.zeros((), jnp.int32)
    stream_start = (running - counts)[0]
    base_row = (device_index - 1) * rows_here
    params = jnp.concatenate(
        [band_bounds.reshape(-1).astype(jnp.int32),
         jnp.stack([stream_start, counts[0], base_row, key_slot]).astype(jnp.int32)]
    )
    return coarse_attention(coarse_queries, near_pair, params, slopes)


def solution(mesh):
    return jax.shard_map(
        on_device,
        mesh=mesh,
        in_specs=(
            P(("groups", "ctx"), None),
            P(("groups", "ctx"), None),
            P(("groups", "ctx"), None),
            P(("groups", "ctx"), None),
            P("ctx", None),
            P(),
            P("ctx", None),
            P("ctx", None),
            P(),
            P(("groups", "ctx"), None),
            P(("groups", "ctx")),
            P(("groups", "ctx"), None),
        ),
        out_specs=P(("groups", "ctx"), None),
        check_vma=False,
    )
```

```python
import functools

import jax
import jax.numpy as jnp
from jax import lax
from jax.experimental import pallas as pl
from jax.experimental.pallas import tpu as pltpu
from jax.sharding import PartitionSpec as P

HEADS = 8
HEAD_DIM = 128
W = 512
BAND = 512
CB = 256


NEG_FILL = -1e30


def passed_along(array, axis, by):
    length = lax.axis_size(axis)
    pairs = [(i, i + by) for i in range(length) if 0 <= i + by < length]
    return lax.ppermute(array, axis, pairs)


def with_halo(array, sides, width):
    for axis, dim in sides:
        size, length = (lax.axis_size(axis), array.shape[dim])
        up = [(i, (i + 1) % size) for i in range(size - 1)]
        down = [(j, i) for i, j in up]
        last = lax.slice_in_dim(array, length - width, length, axis=dim)
        first = lax.slice_in_dim(array, 0, width, axis=dim)
        before = lax.ppermute(last, axis, up)
        after = lax.ppermute(first, axis, down)
        array = jnp.concatenate([before, array, after], axis=dim)
    return array


def sent_to(array, group_flip, ctx_step):
    groups, length = (lax.axis_size("groups"), lax.axis_size("ctx"))
    pairs = [
        (g * length + c, (g ^ group_flip) * length + c + ctx_step)
        for g in range(groups)
        for c in range(length)
        if 0 <= c + ctx_step < length
    ]
    return lax.ppermute(array, ("groups", "ctx"), pairs)


def head_split(matrix):
    return matrix.reshape(matrix.shape[0], HEADS, HEAD_DIM)


def attend(queries, key_rows, value_rows, allowed, time_bias):
    scores = jnp.einsum(
        "qhd,khd->hqk",
        head_split(queries),
        head_split(key_rows),
        preferred_element_type=jnp.float32,
    ) * HEAD_DIM ** (-0.5)
    scores = jnp.where(allowed[None], scores + time_bias, NEG_FILL)
    largest = jnp.max(scores, axis=2, keepdims=True)
    exponent = jnp.exp(scores - largest)
    weights = (exponent / jnp.sum(exponent, axis=2, keepdims=True)).astype(jnp.bfloat16)
    blended = jnp.einsum(
        "hqk,khd->qhd", weights, head_split(value_rows), preferred_element_type=jnp.float32
    )
    return blended.reshape(queries.shape[0], -1)


def normalize(sem_stream, norm_gain):
    scaled = sem_stream * lax.rsqrt(
        jnp.mean(sem_stream * sem_stream, axis=1, keepdims=True) + 1e-05
    )
    return (scaled * norm_gain[None, :]).astype(jnp.bfloat16)


def contract_rows(left_side, weight_piece):
    return jnp.dot(left_side, weight_piece, preferred_element_type=jnp.float32)


def coarse_kernel(prm, slopes_ref, q_ref, k_ref, v_ref, o_ref, *, blocks, near_rows, span):
    n = pl.program_id(0)
    band_low = prm[2 * n]
    band_high = prm[2 * n + 1]
    stream_start = prm[2 * blocks]
    live_count = prm[2 * blocks + 1]
    base_row = prm[2 * blocks + 2]
    first_key = jnp.minimum(band_low - base_row, near_rows - BAND)
    step = span - BAND
    window = pl.multiple_of(jnp.clip(first_key // step * step, 0, near_rows - span), step)
    rows = n * CB + lax.broadcasted_iota(jnp.int32, (1, CB), 1)
    timing = ((stream_start + rows) // 2).astype(jnp.float32) * (2.0 / 3.0)
    key_global = base_row + window + lax.broadcasted_iota(jnp.int32, (span, 1), 0)
    inside = (key_global >= band_low) & (key_global < band_high)
    distance = jnp.where(inside, jnp.abs(timing - key_global.astype(jnp.float32)), -NEG_FILL)
    live_rows = n * CB + lax.broadcasted_iota(jnp.int32, (CB, 1), 0) < live_count
    for h in range(HEADS):
        cols = slice(h * HEAD_DIM, (h + 1) * HEAD_DIM)
        scores = lax.dot_general(
            k_ref[pl.ds(window, span), cols], q_ref[:, cols], (((1,), (1,)), ((), ())),
            preferred_element_type=jnp.float32,
        ) * HEAD_DIM ** (-0.5)
        scores = scores + distance * (-slopes_ref[h] / BAND)
        largest = jnp.max(scores, axis=0, keepdims=True)
        exponent = jnp.exp(scores - largest)
        total = jnp.sum(exponent, axis=0, keepdims=True)
        weights = (exponent * (1.0 / total)).astype(jnp.bfloat16)
        blended = lax.dot_general(
            weights, v_ref[pl.ds(window, span), cols], (((0,), (0,)), ((), ())),
            preferred_element_type=jnp.float32,
        )
        o_ref[:, cols] = jnp.where(live_rows, blended, 0.0).astype(jnp.bfloat16)


def coarse_attention(coarse_queries, near_pair, params, slopes):
    slots, width = coarse_queries.shape
    blocks = slots // CB
    near_rows = near_pair.shape[1]
    kernel = functools.partial(coarse_kernel, blocks=blocks, near_rows=near_rows, span=BAND + 128)
    grid_spec = pltpu.PrefetchScalarGridSpec(
        num_scalar_prefetch=1,
        grid=(blocks,),
        in_specs=[
            pl.BlockSpec(memory_space=pltpu.SMEM),
            pl.BlockSpec((CB, width), lambda n, prm: (n, 0)),
            pl.BlockSpec((None, near_rows, width), lambda n, prm: (prm[2 * blocks + 3], 0, 0)),
            pl.BlockSpec((None, near_rows, width), lambda n, prm: (1 - prm[2 * blocks + 3], 0, 0)),
        ],
        out_specs=pl.BlockSpec((CB, width), lambda n, prm: (n, 0)),
    )
    return pl.pallas_call(
        kernel,
        grid_spec=grid_spec,
        out_shape=jax.ShapeDtypeStruct((slots, width), jnp.bfloat16),
        compiler_params=pltpu.CompilerParams(dimension_semantics=("arbitrary",)),
    )(params, slopes, coarse_queries, near_pair, near_pair)


def on_device(
    sem_queries,
    sem_keys,
    sem_values,
    sem_inputs,
    out_proj,
    norm_gain,
    key_proj,
    value_proj,
    slopes,
    coarse_queries,
    counts,
    band_bounds,
):
    rows_here = sem_queries.shape[0]
    device_index = lax.axis_index("ctx")
    ctx_size = lax.axis_size("ctx")
    full_out_proj = lax.all_gather(out_proj, "ctx", axis=0, tiled=True)
    running = counts
    reach = 1
    while reach < ctx_size:
        running = running + passed_along(running, "ctx", reach)
        reach *= 2
    group_size = lax.axis_size("groups")
    shared = group_size % 2 == 0
    if shared:
        partners = [(i, i ^ 1) for i in range(group_size)]
        key_side = lax.axis_index("groups") % 2 == 0
        own_proj = jnp.where(key_side, key_proj, value_proj)
        gathered_proj = lax.all_gather(own_proj, "ctx", axis=0, tiled=True)
    else:
        stacked_proj = jnp.stack([key_proj, value_proj])
        gathered_proj = lax.all_gather(stacked_proj, "ctx", axis=1, tiled=True)
    own_pair = jnp.stack([sem_keys, sem_values])
    reach_shards = (W - 1 + rows_here - 1) // rows_here
    earlier = []
    relayed = own_pair
    for distance in range(1, reach_shards + 1):
        if distance == 2:
            full_out_proj, relayed = lax.optimization_barrier((full_out_proj, relayed))
        relayed = passed_along(relayed, "ctx", 1)
        earlier.insert(0, relayed)
    window_pair = jnp.concatenate(earlier + [own_pair], axis=1)
    query_pos = jnp.arange(rows_here, dtype=jnp.int32)
    key_pos = jnp.arange(window_pair.shape[1], dtype=jnp.int32)
    key_lag = query_pos[:, None] + reach_shards * rows_here - key_pos[None, :]
    key_global = device_index * rows_here - reach_shards * rows_here + key_pos
    allowed = (key_lag >= 0) & (key_lag < W) & (key_global[None, :] >= 0)
    sem_att = attend(sem_queries, window_pair[0], window_pair[1], allowed, 0.0).astype(jnp.bfloat16)
    running, sem_att = lax.optimization_barrier((running, sem_att))
    projected = contract_rows(sem_att, full_out_proj)
    sem_stream = sem_inputs.astype(jnp.float32) + projected
    normed = normalize(sem_stream, norm_gain)
    if shared:
        partner_normed = lax.ppermute(normed, "groups", partners)
        partner_part = contract_rows(partner_normed, gathered_proj).astype(jnp.bfloat16)
        partner_sum = sent_to(partner_part, 1, 0)
        other_pieces = [sent_to(partner_sum, 0, 1), partner_sum, sent_to(partner_sum, 0, -1)]
        own_sum = contract_rows(normed, gathered_proj).astype(jnp.bfloat16)
        mine_pieces = [sent_to(own_sum, 0, 1), own_sum, sent_to(own_sum, 0, -1)]
        near_pair = jnp.concatenate(mine_pieces + other_pieces, axis=0).reshape(
            2, 3 * rows_here, own_sum.shape[1])
        key_slot = jnp.where(key_side, 0, 1)
    else:
        cross_keys = contract_rows(normed, gathered_proj[0]).astype(jnp.bfloat16)
        cross_values = contract_rows(normed, gathered_proj[1]).astype(jnp.bfloat16)
        near_pair = with_halo(jnp.stack([cross_keys, cross_values]), (("ctx", 1),), rows_here)
        key_slot = jnp.zeros((), jnp.int32)
    stream_start = (running - counts)[0]
    base_row = (device_index - 1) * rows_here
    params = jnp.concatenate(
        [band_bounds.reshape(-1).astype(jnp.int32),
         jnp.stack([stream_start, counts[0], base_row, key_slot]).astype(jnp.int32)]
    )
    return coarse_attention(coarse_queries, near_pair, params, slopes)


def solution(mesh):
    return jax.shard_map(
        on_device,
        mesh=mesh,
        in_specs=(
            P(("groups", "ctx"), None),
            P(("groups", "ctx"), None),
            P(("groups", "ctx"), None),
            P(("groups", "ctx"), None),
            P("ctx", None),
            P(),
            P("ctx", None),
            P("ctx", None),
            P(),
            P(("groups", "ctx"), None),
            P(("groups", "ctx")),
            P(("groups", "ctx"), None),
        ),
        out_specs=P(("groups", "ctx"), None),
        check_vma=False,
    )
```

```python
import functools

import jax
import jax.numpy as jnp
from jax import lax
from jax.experimental import pallas as pl
from jax.experimental.pallas import tpu as pltpu
from jax.sharding import PartitionSpec as P

HEADS = 8
HEAD_DIM = 128
W = 512
BAND = 512
CB = 256


NEG_FILL = -1e30


def passed_along(array, axis, by):
    length = lax.axis_size(axis)
    pairs = [(i, i + by) for i in range(length) if 0 <= i + by < length]
    return lax.ppermute(array, axis, pairs)


def with_halo(array, sides, width):
    for axis, dim in sides:
        size, length = (lax.axis_size(axis), array.shape[dim])
        up = [(i, (i + 1) % size) for i in range(size - 1)]
        down = [(j, i) for i, j in up]
        last = lax.slice_in_dim(array, length - width, length, axis=dim)
        first = lax.slice_in_dim(array, 0, width, axis=dim)
        before = lax.ppermute(last, axis, up)
        after = lax.ppermute(first, axis, down)
        array = jnp.concatenate([before, array, after], axis=dim)
    return array


def sent_to(array, group_flip, ctx_step):
    groups, length = (lax.axis_size("groups"), lax.axis_size("ctx"))
    pairs = [
        (g * length + c, (g ^ group_flip) * length + c + ctx_step)
        for g in range(groups)
        for c in range(length)
        if 0 <= c + ctx_step < length
    ]
    return lax.ppermute(array, ("groups", "ctx"), pairs)


def head_split(matrix):
    return matrix.reshape(matrix.shape[0], HEADS, HEAD_DIM)


def attend(queries, key_rows, value_rows, allowed, time_bias):
    scores = jnp.einsum(
        "qhd,khd->hqk",
        head_split(queries),
        head_split(key_rows),
        preferred_element_type=jnp.float32,
    ) * HEAD_DIM ** (-0.5)
    scores = jnp.where(allowed[None], scores + time_bias, NEG_FILL)
    largest = jnp.max(scores, axis=2, keepdims=True)
    exponent = jnp.exp(scores - largest)
    weights = (exponent / jnp.sum(exponent, axis=2, keepdims=True)).astype(jnp.bfloat16)
    blended = jnp.einsum(
        "hqk,khd->qhd", weights, head_split(value_rows), preferred_element_type=jnp.float32
    )
    return blended.reshape(queries.shape[0], -1)


def normalize(sem_stream, norm_gain):
    scaled = sem_stream * lax.rsqrt(
        jnp.mean(sem_stream * sem_stream, axis=1, keepdims=True) + 1e-05
    )
    return (scaled * norm_gain[None, :]).astype(jnp.bfloat16)


def contract_rows(left_side, weight_piece):
    return jnp.dot(left_side, weight_piece, preferred_element_type=jnp.float32)


def coarse_kernel(prm, slopes_ref, q_ref, k_ref, v_ref, o_ref, *, blocks, near_rows, span):
    n = pl.program_id(0)
    band_low = prm[2 * n]
    band_high = prm[2 * n + 1]
    stream_start = prm[2 * blocks]
    live_count = prm[2 * blocks + 1]
    base_row = prm[2 * blocks + 2]
    first_key = jnp.minimum(band_low - base_row, near_rows - BAND)
    step = span - BAND
    window = pl.multiple_of(jnp.clip(first_key // step * step, 0, near_rows - span), step)
    rows = n * CB + lax.broadcasted_iota(jnp.int32, (1, CB), 1)
    timing = ((stream_start + rows) // 2).astype(jnp.float32) * (2.0 / 3.0)
    key_global = base_row + window + lax.broadcasted_iota(jnp.int32, (span, 1), 0)
    inside = (key_global >= band_low) & (key_global < band_high)
    distance = jnp.where(inside, jnp.abs(timing - key_global.astype(jnp.float32)), -NEG_FILL)
    live_rows = n * CB + lax.broadcasted_iota(jnp.int32, (CB, 1), 0) < live_count
    for h in range(HEADS):
        cols = slice(h * HEAD_DIM, (h + 1) * HEAD_DIM)
        scores = lax.dot_general(
            k_ref[pl.ds(window, span), cols], q_ref[:, cols], (((1,), (1,)), ((), ())),
            preferred_element_type=jnp.float32,
        ) * HEAD_DIM ** (-0.5)
        scores = scores + distance * (-slopes_ref[h] / BAND)
        largest = jnp.max(scores, axis=0, keepdims=True)
        exponent = jnp.exp(scores - largest)
        total = jnp.sum(exponent, axis=0, keepdims=True)
        weights = (exponent * (1.0 / total)).astype(jnp.bfloat16)
        blended = lax.dot_general(
            weights, v_ref[pl.ds(window, span), cols], (((0,), (0,)), ((), ())),
            preferred_element_type=jnp.float32,
        )
        o_ref[:, cols] = jnp.where(live_rows, blended, 0.0).astype(jnp.bfloat16)


def coarse_attention(coarse_queries, near_pair, params, slopes):
    slots, width = coarse_queries.shape
    blocks = slots // CB
    near_rows = near_pair.shape[1]
    kernel = functools.partial(coarse_kernel, blocks=blocks, near_rows=near_rows, span=BAND + 128)
    grid_spec = pltpu.PrefetchScalarGridSpec(
        num_scalar_prefetch=1,
        grid=(blocks,),
        in_specs=[
            pl.BlockSpec(memory_space=pltpu.SMEM),
            pl.BlockSpec((CB, width), lambda n, prm: (n, 0)),
            pl.BlockSpec((None, near_rows, width), lambda n, prm: (prm[2 * blocks + 3], 0, 0)),
            pl.BlockSpec((None, near_rows, width), lambda n, prm: (1 - prm[2 * blocks + 3], 0, 0)),
        ],
        out_specs=pl.BlockSpec((CB, width), lambda n, prm: (n, 0)),
    )
    return pl.pallas_call(
        kernel,
        grid_spec=grid_spec,
        out_shape=jax.ShapeDtypeStruct((slots, width), jnp.bfloat16),
        compiler_params=pltpu.CompilerParams(dimension_semantics=("arbitrary",)),
    )(params, slopes, coarse_queries, near_pair, near_pair)


def on_device(
    sem_queries,
    sem_keys,
    sem_values,
    sem_inputs,
    out_proj,
    norm_gain,
    key_proj,
    value_proj,
    slopes,
    coarse_queries,
    counts,
    band_bounds,
):
    rows_here = sem_queries.shape[0]
    device_index = lax.axis_index("ctx")
    ctx_size = lax.axis_size("ctx")
    full_out_proj = lax.all_gather(out_proj, "ctx", axis=0, tiled=True)
    running = counts
    reach = 1
    while reach < ctx_size:
        running = running + passed_along(running, "ctx", reach)
        reach *= 2
    group_size = lax.axis_size("groups")
    shared = group_size % 2 == 0
    if shared:
        partners = [(i, i ^ 1) for i in range(group_size)]
        key_side = lax.axis_index("groups") % 2 == 0
        own_proj = jnp.where(key_side, key_proj, value_proj)
        gathered_proj = lax.all_gather(own_proj, "ctx", axis=0, tiled=True)
    else:
        stacked_proj = jnp.stack([key_proj, value_proj])
        gathered_proj = lax.all_gather(stacked_proj, "ctx", axis=1, tiled=True)
    own_pair = jnp.stack([sem_keys, sem_values])
    reach_shards = (W - 1 + rows_here - 1) // rows_here
    earlier = []
    relayed = own_pair
    for distance in range(1, reach_shards + 1):
        if distance == 2:
            full_out_proj, relayed = lax.optimization_barrier((full_out_proj, relayed))
        relayed = passed_along(relayed, "ctx", 1)
        earlier.insert(0, relayed)
    window_pair = jnp.concatenate(earlier + [own_pair], axis=1)
    query_pos = jnp.arange(rows_here, dtype=jnp.int32)
    key_pos = jnp.arange(window_pair.shape[1], dtype=jnp.int32)
    key_lag = query_pos[:, None] + reach_shards * rows_here - key_pos[None, :]
    key_global = device_index * rows_here - reach_shards * rows_here + key_pos
    allowed = (key_lag >= 0) & (key_lag < W) & (key_global[None, :] >= 0)
    sem_att = attend(sem_queries, window_pair[0], window_pair[1], allowed, 0.0).astype(jnp.bfloat16)
    projected = contract_rows(sem_att, full_out_proj)
    sem_stream = sem_inputs.astype(jnp.float32) + projected
    normed = normalize(sem_stream, norm_gain)
    if shared:
        partner_normed = lax.ppermute(normed, "groups", partners)
        running, partner_normed = lax.optimization_barrier((running, partner_normed))
        partner_part = contract_rows(partner_normed, gathered_proj).astype(jnp.bfloat16)
        partner_sum = sent_to(partner_part, 1, 0)
        other_pieces = [sent_to(partner_sum, 0, 1), partner_sum, sent_to(partner_sum, 0, -1)]
        own_sum = contract_rows(normed, gathered_proj).astype(jnp.bfloat16)
        mine_pieces = [sent_to(own_sum, 0, 1), own_sum, sent_to(own_sum, 0, -1)]
        near_pair = jnp.concatenate(mine_pieces + other_pieces, axis=0).reshape(
            2, 3 * rows_here, own_sum.shape[1])
        key_slot = jnp.where(key_side, 0, 1)
    else:
        cross_keys = contract_rows(normed, gathered_proj[0]).astype(jnp.bfloat16)
        cross_values = contract_rows(normed, gathered_proj[1]).astype(jnp.bfloat16)
        near_pair = with_halo(jnp.stack([cross_keys, cross_values]), (("ctx", 1),), rows_here)
        key_slot = jnp.zeros((), jnp.int32)
    stream_start = (running - counts)[0]
    base_row = (device_index - 1) * rows_here
    params = jnp.concatenate(
        [band_bounds.reshape(-1).astype(jnp.int32),
         jnp.stack([stream_start, counts[0], base_row, key_slot]).astype(jnp.int32)]
    )
    return coarse_attention(coarse_queries, near_pair, params, slopes)


def solution(mesh):
    return jax.shard_map(
        on_device,
        mesh=mesh,
        in_specs=(
            P(("groups", "ctx"), None),
            P(("groups", "ctx"), None),
            P(("groups", "ctx"), None),
            P(("groups", "ctx"), None),
            P("ctx", None),
            P(),
            P("ctx", None),
            P("ctx", None),
            P(),
            P(("groups", "ctx"), None),
            P(("groups", "ctx")),
            P(("groups", "ctx"), None),
        ),
        out_specs=P(("groups", "ctx"), None),
        check_vma=False,
    )
```
